32 devices in a mesh: tile: 8 (over z, x), lev: 4 (over y, core).
Axes of the slice: x: 2, y: 2, z: 4, core: 2. Of those that a mesh axis runs over, the one named last changes fastest.
Arguments:
- obs_adjoint: float32 [16, 4096], P('lev', 'tile'), may hold values from -6 to 6
- foot_obs: int32 [8, 8, 128], P('tile'), may hold values from 0 to 511
- foot_cell: int32 [8, 8, 128], P('tile'), may hold values from 0 to 4095
- foot_weight: float32 [8, 8, 128], P('tile'), may hold values from 0.2 to 1
- counts: int32 [8, 8], P('tile'), may hold values from 0 to 128, as said below
- ensemble: bfloat16 [16, 80, 128, 256], P('lev', None, 'tile'), may hold values from -6 to 6
- vert_root: bfloat16 [16, 16], replicated, may hold values from -0.5 to 3
- radius: int32 [16], P('lev'), may hold values from 1 to 16, as said below
- alpha: float32 [16, 80, 128, 256], P('lev', None, 'tile'), may hold values from -32 to 32
Outputs:
- gradient: float32 [16, 80, 128, 256], P('lev', None, 'tile')
- r_factor: float32 [80, 80], replicated
The draws below stay inside these ranges and needn't reach their ends.
Inputs may be any that keep to these rules, and one draw needn't show every extreme that they name: The live slots of a block are its first counts[s, d] slots. In every draw some destination tile has 128 live slots from every sender tile. Some level group has radius 16 in every draw.
All inputs are finite; a program needn't handle non-finite values.
Results may differ from the reference program's by a relative error of at most 0.0003.
The reference program's roundings to bfloat16 on the way count: a program that leaves them out, or rounds other values in their place, can miss the bound.
Values may be sent and summed in bfloat16 or wider, within the bound.
No kernel may reach another device: no remote copies, remote signals or barrier semaphores. Data moves between devices by JAX's collectives and lax.ppermute only.
A program may use at most 128 MiB of HBM per device.

```python
import math
import jax
import jax.numpy as jnp
from jax import lax

M = 80
CX = 16
CY = 256
HALO = 16
CAP = 128
OBS_DEV = 512
TILES = 8
NLEV = 16
NX = 128
OBS = 4096


def draw_counts(key, part):
    key_one, key_two, key_three = jax.random.split(key, 3)
    floor_dest = jax.random.randint(key_one, (TILES,), 0, CAP)
    counts = jax.random.randint(key_two, (TILES, TILES), floor_dest[None, :], CAP + 1)
    full_dest = jax.random.randint(key_three, (), 0, TILES)
    column = lax.broadcasted_iota(jnp.int32, (TILES, TILES), 1)
    return jnp.where(column == full_dest, CAP, counts).astype(jnp.int32)


def draw_radius(key, part):
    key_one, key_two = jax.random.split(key, 2)
    radius = jax.random.randint(key_one, (NLEV,), 1, HALO + 1)
    widest = jax.random.randint(key_two, (), 0, NLEV)
    level_index = lax.broadcasted_iota(jnp.int32, (NLEV,), 0)
    return jnp.where(level_index == widest, HALO, radius).astype(jnp.int32)


def draw_vert_root(key, part):
    key_one, key_two = jax.random.split(key, 2)
    diagonal = jax.random.uniform(key_one, (NLEV,), jnp.float32, 1.5, 2.5)
    offdiag = jax.random.uniform(key_two, (NLEV, NLEV), jnp.float32, -0.3, 0.3)
    row_index = lax.broadcasted_iota(jnp.int32, (NLEV, NLEV), 0)
    col_index = lax.broadcasted_iota(jnp.int32, (NLEV, NLEV), 1)
    matrix = jnp.where(row_index == col_index, diagonal[None, :], offdiag)
    return matrix.astype(jnp.bfloat16)


def draw_alpha(key, part):
    key_one, key_two, key_three = jax.random.split(key, 3)
    shape = (NLEV, M, NX, CY)
    member_scale = 0.2 * jnp.exp(jax.random.uniform(key_one, (M,), jnp.float32, 0.0, math.log(10.0)))
    x_index = lax.broadcasted_iota(jnp.float32, (1, 1, NX, 1), 2)
    column_scale = 0.5 * jnp.power(3.0, x_index / NX)
    column_scale = column_scale * jnp.exp(jax.random.uniform(key_two, (NLEV, 1, NX, 1), jnp.float32, 0.0, math.log(3.4)))
    base = jnp.clip(jax.random.normal(key_three, shape, jnp.float32), -3.0, 3.0)
    return base * member_scale[None, :, None, None] * column_scale


def place_ends(values, rng, least, top_value):
    place = [jax.random.randint(jax.random.fold_in(rng, axis), (), 0, length) for axis, length in enumerate(values.shape)]
    main_axis = values.shape.index(max(values.shape))
    neighbour = place[:main_axis] + [(place[main_axis] + 1) % values.shape[main_axis]] + place[main_axis + 1:]
    return values.at[tuple(place)].set(least).at[tuple(neighbour)].set(top_value)


def level_of(own_key, dims, cuts, smallest, largest):
    gain = 1.0
    for dim, parts in cuts:
        draws = jax.random.uniform(jax.random.fold_in(jax.random.fold_in(own_key, 6), dim), (parts,), jnp.float32, smallest / len(cuts), largest / len(cuts))
        gain = gain * jnp.repeat(jnp.exp(draws), dims[dim] // parts).reshape((-1,) + (1,) * (len(dims) - 1 - dim))
    return gain


def bell_draw(own_key, dims, spread, reach, pieces=(), kind=jnp.bfloat16):
    factor_of = level_of(own_key, dims, pieces, -0.22, 0.18) if pieces else 1.0
    result = jax.random.normal(own_key, dims, jnp.float32) * spread * factor_of
    return jnp.minimum(jnp.maximum(result, -reach), reach).astype(kind)


def setup_inputs(seed: int = 0) -> dict:
    splits = jax.random.split(jax.random.key(seed), 10)
    obs_adjoint = bell_draw(splits[0], (NLEV, OBS), 1.0, 6.0, ((0, 4), (1, 8)), jnp.float32)
    foot_obs = place_ends(jax.random.randint(splits[1], (TILES, TILES, CAP), 0, OBS_DEV), jax.random.fold_in(splits[1], 1), 0, OBS_DEV - 1).astype(jnp.int32)
    foot_cell = place_ends(jax.random.randint(splits[2], (TILES, TILES, CAP), 0, CX * CY), jax.random.fold_in(splits[2], 1), 0, (CX * CY) - 1).astype(jnp.int32)
    foot_weight = jnp.clip(0.2 + 0.8 * jax.random.uniform(splits[3], (TILES, TILES, CAP), jnp.float32) ** level_of(splits[3], (TILES, TILES, CAP), ((0, 8),), -0.2, 0.2), 0.2, 1.0)
    counts = draw_counts(jax.random.fold_in(splits[9], 71), 0)
    ensemble = bell_draw(splits[5], (NLEV, M, NX, CY), 1.0, 6.0, ((0, 4), (2, 8)))
    vert_root = draw_vert_root(jax.random.fold_in(splits[9], 71), 0)
    radius = draw_radius(jax.random.fold_in(splits[9], 71), 0)
    alpha = draw_alpha(jax.random.fold_in(splits[9], 71), 0)
    return dict(obs_adjoint=obs_adjoint, foot_obs=foot_obs, foot_cell=foot_cell, foot_weight=foot_weight, counts=counts, ensemble=ensemble, vert_root=vert_root, radius=radius, alpha=alpha)


def taps_table(radius, offsets):
    reach_max = radius.astype(jnp.float32)[:, None, None]
    distance = jnp.abs(offsets).astype(jnp.float32)[None]
    weights = jnp.where(distance <= reach_max, (reach_max + 1.0 - distance) / (reach_max + 1.0), 0.0)
    return weights.astype(jnp.bfloat16)

def reference(obs_adjoint, foot_obs, foot_cell, foot_weight, counts, ensemble, vert_root, radius, alpha):
    shape = (TILES, TILES, CAP)
    slot_index = lax.broadcasted_iota(jnp.int32, shape, 2)
    sender = lax.broadcasted_iota(jnp.int32, shape, 0)
    destination = lax.broadcasted_iota(jnp.int32, shape, 1)
    live_mask = (slot_index < counts[:, :, None]).astype(jnp.int32)
    source_index = (sender * OBS_DEV + foot_obs).reshape(-1).astype(jnp.int32)
    values = jnp.take(obs_adjoint, source_index, axis=1).reshape(NLEV, TILES, TILES, CAP)
    payload = values * (foot_weight * live_mask.astype(jnp.float32))[None]
    target = (destination * (CX * CY) + foot_cell).reshape(-1).astype(jnp.int32)
    forcing = jnp.zeros((NLEV, NX * CY), jnp.float32).at[:, target].add(payload.reshape(NLEV, -1))
    forcing = forcing.reshape(NLEV, NX, CY)
    member_forcing = (ensemble.astype(jnp.float32) * forcing[:, None]).astype(jnp.bfloat16)
    level_mix = jnp.einsum('lk,lmxy->kmxy', vert_root.astype(jnp.float32), member_forcing.astype(jnp.float32))
    level_mix = level_mix.astype(jnp.bfloat16)
    row_iota = jnp.arange(CY, dtype=jnp.int32)
    col_iota = jnp.arange(NX, dtype=jnp.int32)
    taps_rows = taps_table(radius, row_iota[:, None] - row_iota[None, :])
    taps_cols = taps_table(radius, col_iota[:, None] - col_iota[None, :])

    def per_level(level_args):
        mix_level, rows_level, cols_level, alpha_level = level_args
        smooth_y = jnp.einsum('mxy,yz->mxz', mix_level.astype(jnp.float32), rows_level.astype(jnp.float32))
        smooth_y = smooth_y.astype(jnp.bfloat16)
        smooth_x = jnp.einsum('mey,ex->mxy', smooth_y.astype(jnp.float32), cols_level.astype(jnp.float32))
        return alpha_level + smooth_x
    gradient = lax.map(per_level, (level_mix, taps_rows, taps_cols, alpha))
    gram = jnp.einsum('kmxy,knxy->mn', gradient, gradient, precision=lax.Precision.HIGHEST)
    gram = gram / float(NLEV * NX * CY)
    r_factor = jnp.linalg.cholesky(gram).T
    return (gradient, r_factor)
```

```python
import jax
import jax.numpy as jnp
from jax import lax
from jax.sharding import PartitionSpec as P

HALO = 16


def taps_table(radius, offsets):
    reach_max = radius.astype(jnp.float32)[:, None, None]
    distance = jnp.abs(offsets).astype(jnp.float32)[None]
    weights = jnp.where(
        distance <= reach_max, (reach_max + 1.0 - distance) / (reach_max + 1.0), 0.0
    )
    return weights.astype(jnp.bfloat16)


def first_hits(cells):
    slots = cells.shape[-1]
    same = cells[..., :, None] == cells[..., None, :]
    later = lax.broadcasted_iota(jnp.int32, (slots, slots), 1) < lax.broadcasted_iota(
        jnp.int32, (slots, slots), 0
    )
    return jnp.logical_not(jnp.any(same & later, axis=-1))


def one_hot(cells, keep, cell_count):
    grid = lax.broadcasted_iota(jnp.int32, cells.shape + (cell_count,), cells.ndim)
    hit = (cells[..., None] == grid) & keep[..., None]
    return hit.astype(jnp.bfloat16)


def shards(
    obs_adjoint, foot_obs, foot_cell, foot_weight, counts, ensemble, vert_root, radius, alpha
):
    lev_dev, members, col_count, row_count = alpha.shape
    tile_count = lax.axis_size("tile")
    group_count = lax.axis_size("lev")
    capacity = foot_obs.shape[2]
    cell_count = col_count * row_count
    slots = tile_count * capacity
    packed = slots < cell_count
    assert HALO <= col_count
    tile = lax.axis_index("tile")

    slot_index = lax.broadcasted_iota(jnp.int32, (tile_count, capacity), 1)
    live_mask = (slot_index < counts[0][:, None]).astype(jnp.float32)
    values = jnp.take(obs_adjoint, foot_obs[0], axis=1)
    payload = values * (foot_weight[0] * live_mask)[None]
    arrived = lax.all_to_all(payload, "tile", split_axis=1, concat_axis=1, tiled=True)
    all_cells = lax.all_gather(foot_cell[0], "tile")
    cells_of = jnp.swapaxes(all_cells, 0, 1).reshape(tile_count, slots)
    cell_index = lax.dynamic_index_in_dim(cells_of, tile, 0, keepdims=False)

    forcing = jnp.zeros((lev_dev, cell_count), jnp.float32)
    forcing = forcing.at[:, cell_index].add(arrived.reshape(lev_dev, -1))
    forcing = forcing.reshape(lev_dev, col_count, row_count)
    member_forcing = (ensemble * forcing[:, None]).astype(jnp.bfloat16)
    member_forcing = member_forcing.reshape(lev_dev, members, cell_count)

    if packed:
        near = jnp.stack(
            [
                lax.dynamic_index_in_dim(cells_of, jnp.maximum(tile - 1, 0), 0, keepdims=False),
                cell_index,
                lax.dynamic_index_in_dim(
                    cells_of, jnp.minimum(tile + 1, tile_count - 1), 0, keepdims=False
                ),
            ]
        )
        hits = one_hot(near, first_hits(near), cell_count)
        member_forcing = jnp.einsum(
            "lmc,sc->lms", member_forcing, hits[1], preferred_element_type=jnp.float32
        ).astype(jnp.bfloat16)

    regrouped = lax.all_to_all(member_forcing, "lev", split_axis=1, concat_axis=0, tiled=True)
    local_mix = jnp.einsum(
        "lk,lmc->kmc", vert_root, regrouped, preferred_element_type=jnp.float32
    )
    level_mix = lax.all_to_all(
        local_mix.astype(jnp.bfloat16), "lev", split_axis=0, concat_axis=1, tiled=True
    )
    ends = tile_count - 1
    from_left = lax.ppermute(level_mix, "tile", [(i, i + 1) for i in range(ends)])
    from_right = lax.ppermute(level_mix, "tile", [(i + 1, i) for i in range(ends)])
    three = jnp.stack([from_left, level_mix, from_right])
    if packed:
        three = jnp.einsum(
            "tkms,tsc->kmtc", three, hits, preferred_element_type=jnp.float32
        ).astype(jnp.bfloat16)
    else:
        three = jnp.moveaxis(three, 0, 2)
    wide_mix = three.reshape(lev_dev, members, 3 * col_count, row_count)

    row_iota = jnp.arange(row_count, dtype=jnp.int32)
    taps_rows = taps_table(radius, row_iota[:, None] - row_iota[None, :])
    wide_iota = jnp.arange(3 * col_count, dtype=jnp.int32)
    col_iota = jnp.arange(col_count, dtype=jnp.int32)
    taps_cols = taps_table(radius, wide_iota[:, None] - col_count - col_iota[None, :])
    smooth_wide = jnp.einsum(
        "kmxy,kyz->kmxz", wide_mix, taps_rows, preferred_element_type=jnp.float32
    ).astype(jnp.bfloat16)
    smooth_x = jnp.einsum(
        "kmey,kex->kmxy", smooth_wide, taps_cols, preferred_element_type=jnp.float32
    )
    gradient = alpha + smooth_x
    panel = gradient.reshape(lev_dev, members, col_count * row_count)
    total_cells = float(lev_dev * group_count * col_count * tile_count * row_count)
    gram_local = (
        jnp.einsum("kmc,knc->mn", panel, panel, precision=lax.Precision.HIGHEST) / total_cells
    )
    gram_total = lax.psum(gram_local, ("tile", "lev"))
    r_factor = jnp.linalg.cholesky(gram_total).T
    return (gradient, r_factor)


def solution(mesh):
    return jax.shard_map(
        shards,
        mesh=mesh,
        in_specs=(
            P("lev", "tile"),
            P("tile", None, None),
            P("tile", None, None),
            P("tile", None, None),
            P("tile", None),
            P("lev", None, "tile", None),
            P(),
            P("lev"),
            P("lev", None, "tile", None),
        ),
        out_specs=(P("lev", None, "tile", None), P()),
        check_vma=False,
    )
```

```python
import jax
import jax.numpy as jnp
from jax import lax
from jax.sharding import PartitionSpec as P

HALO = 16


def taps_table(radius, offsets):
    reach_max = radius.astype(jnp.float32)[:, None, None]
    distance = jnp.abs(offsets).astype(jnp.float32)[None]
    weights = jnp.where(
        distance <= reach_max, (reach_max + 1.0 - distance) / (reach_max + 1.0), 0.0
    )
    return weights.astype(jnp.bfloat16)


def first_hits(cells):
    slots = cells.shape[-1]
    same = cells[..., :, None] == cells[..., None, :]
    later = lax.broadcasted_iota(jnp.int32, (slots, slots), 1) < lax.broadcasted_iota(
        jnp.int32, (slots, slots), 0
    )
    return jnp.logical_not(jnp.any(same & later, axis=-1))


def one_hot(cells, keep, cell_count):
    grid = lax.broadcasted_iota(jnp.int32, cells.shape + (cell_count,), cells.ndim)
    hit = (cells[..., None] == grid) & keep[..., None]
    return hit.astype(jnp.bfloat16)


def shards(
    obs_adjoint, foot_obs, foot_cell, foot_weight, counts, ensemble, vert_root, radius, alpha
):
    lev_dev, members, col_count, row_count = alpha.shape
    tile_count = lax.axis_size("tile")
    group_count = lax.axis_size("lev")
    capacity = foot_obs.shape[2]
    cell_count = col_count * row_count
    slots = tile_count * capacity
    packed = slots < cell_count
    assert HALO <= col_count

    slot_index = lax.broadcasted_iota(jnp.int32, (tile_count, capacity), 1)
    live_mask = (slot_index < counts[0][:, None]).astype(jnp.float32)
    values = jnp.take(obs_adjoint, foot_obs[0], axis=1)
    payload = values * (foot_weight[0] * live_mask)[None]
    own_cells = foot_cell[0]
    prev_cells = jnp.concatenate([own_cells[:1], own_cells[:-1]], axis=0)
    next_cells = jnp.concatenate([own_cells[1:], own_cells[-1:]], axis=0)
    cell_rows = jnp.stack([prev_cells, own_cells, next_cells]).astype(jnp.float32)
    outgoing = jnp.concatenate([payload, cell_rows], axis=0)
    arrived = lax.all_to_all(outgoing, "tile", split_axis=1, concat_axis=1, tiled=True)
    near = arrived[lev_dev:].astype(jnp.int32).reshape(3, slots)
    cell_index = near[1]

    forcing = jnp.zeros((lev_dev, cell_count), jnp.float32)
    forcing = forcing.at[:, cell_index].add(arrived[:lev_dev].reshape(lev_dev, -1))
    forcing = forcing.reshape(lev_dev, col_count, row_count)
    member_forcing = (ensemble * forcing[:, None]).astype(jnp.bfloat16)

    if packed:
        keep = first_hits(near)
        hits = one_hot(near, keep, cell_count).reshape(3, slots, col_count, row_count)
        member_forcing = jnp.einsum(
            "lmxy,sxy->lms", member_forcing, hits[1], preferred_element_type=jnp.float32
        ).astype(jnp.bfloat16)

    regrouped = lax.all_to_all(member_forcing, "lev", split_axis=1, concat_axis=0, tiled=True)
    local_mix = jnp.einsum(
        "lk,lm...->km...", vert_root, regrouped, preferred_element_type=jnp.float32
    )
    level_mix = lax.all_to_all(
        local_mix.astype(jnp.bfloat16), "lev", split_axis=0, concat_axis=1, tiled=True
    )
    ends = tile_count - 1
    from_left = lax.ppermute(level_mix, "tile", [(i, i + 1) for i in range(ends)])
    from_right = lax.ppermute(level_mix, "tile", [(i + 1, i) for i in range(ends)])
    three = jnp.stack([from_left, level_mix, from_right])
    if packed:
        three = jnp.einsum(
            "tkms,tsxy->tkmxy", three, hits, preferred_element_type=jnp.float32
        ).astype(jnp.bfloat16)

    row_iota = jnp.arange(row_count, dtype=jnp.int32)
    taps_rows = taps_table(radius, row_iota[:, None] - row_iota[None, :])
    wide_iota = jnp.arange(3 * col_count, dtype=jnp.int32)
    col_iota = jnp.arange(col_count, dtype=jnp.int32)
    taps_cols = taps_table(radius, wide_iota[:, None] - col_count - col_iota[None, :])
    taps_cols = taps_cols.reshape(lev_dev, 3, col_count, col_count)
    smooth_wide = jnp.einsum(
        "tkmxy,kyz->tkmxz", three, taps_rows, preferred_element_type=jnp.float32
    ).astype(jnp.bfloat16)
    smooth_x = jnp.einsum(
        "tkmey,ktex->kmxy", smooth_wide, taps_cols, preferred_element_type=jnp.float32
    )
    gradient = alpha + smooth_x
    total_cells = float(lev_dev * group_count * col_count * tile_count * row_count)
    gram_local = (
        jnp.einsum("kmxy,knxy->mn", gradient, gradient, precision=lax.Precision.HIGHEST) / total_cells
    )
    gram_total = lax.psum(gram_local, ("tile", "lev"))
    r_factor = jnp.linalg.cholesky(gram_total).T
    return (gradient, r_factor)


def solution(mesh):
    return jax.shard_map(
        shards,
        mesh=mesh,
        in_specs=(
            P("lev", "tile"),
            P("tile", None, None),
            P("tile", None, None),
            P("tile", None, None),
            P("tile", None),
            P("lev", None, "tile", None),
            P(),
            P("lev"),
            P("lev", None, "tile", None),
        ),
        out_specs=(P("lev", None, "tile", None), P()),
        check_vma=False,
    )
```

```python
import jax
import jax.numpy as jnp
from jax import lax
from jax.sharding import PartitionSpec as P

HALO = 16


def taps_table(radius, offsets):
    reach_max = radius.astype(jnp.float32)[:, None, None]
    distance = jnp.abs(offsets).astype(jnp.float32)[None]
    weights = jnp.where(
        distance <= reach_max, (reach_max + 1.0 - distance) / (reach_max + 1.0), 0.0
    )
    return weights.astype(jnp.bfloat16)


def first_hits(cells):
    slots = cells.shape[-1]
    same = cells[..., :, None] == cells[..., None, :]
    later = lax.broadcasted_iota(jnp.int32, (slots, slots), 1) < lax.broadcasted_iota(
        jnp.int32, (slots, slots), 0
    )
    return jnp.logical_not(jnp.any(same & later, axis=-1))


def one_hot(cells, keep, cell_count):
    grid = lax.broadcasted_iota(jnp.int32, cells.shape + (cell_count,), cells.ndim)
    hit = (cells[..., None] == grid) & keep[..., None]
    return hit.astype(jnp.bfloat16)


def all_sum(value, axes):
    if any(size & (size - 1) for _, size in axes):
        return lax.psum(value, tuple(name for name, _ in axes))
    for name, size in axes:
        bit = 1
        while bit < size:
            value = value + lax.ppermute(value, name, [(i, i ^ bit) for i in range(size)])
            bit *= 2
    return value


def shards(
    obs_adjoint, foot_obs, foot_cell, foot_weight, counts, ensemble, vert_root, radius, alpha
):
    lev_dev, members, col_count, row_count = alpha.shape
    tile_count = lax.axis_size("tile")
    group_count = lax.axis_size("lev")
    capacity = foot_obs.shape[2]
    cell_count = col_count * row_count
    slots = tile_count * capacity
    packed = slots < cell_count
    assert HALO <= col_count

    slot_index = lax.broadcasted_iota(jnp.int32, (tile_count, capacity), 1)
    live_mask = (slot_index < counts[0][:, None]).astype(jnp.float32)
    values = jnp.take(obs_adjoint, foot_obs[0], axis=1)
    payload = values * (foot_weight[0] * live_mask)[None]
    own_cells = foot_cell[0]
    prev_cells = jnp.concatenate([own_cells[:1], own_cells[:-1]], axis=0)
    next_cells = jnp.concatenate([own_cells[1:], own_cells[-1:]], axis=0)
    cell_rows = jnp.stack([prev_cells, own_cells, next_cells]).astype(jnp.float32)
    outgoing = jnp.concatenate([payload, cell_rows], axis=0)
    arrived = lax.all_to_all(outgoing, "tile", split_axis=1, concat_axis=1, tiled=True)
    near = arrived[lev_dev:].astype(jnp.int32).reshape(3, slots)
    cell_index = near[1]

    if packed:
        same = (cell_index[:, None] == cell_index[None, :]).astype(jnp.float32)
        forcing = jnp.einsum(
            "ls,st->lt", arrived[:lev_dev].reshape(lev_dev, -1), same,
            precision=lax.Precision.HIGHEST,
        )
        keep = first_hits(near)
        hits = one_hot(near, keep, cell_count).reshape(3, slots, col_count, row_count)
        picked = jnp.einsum(
            "lmxy,sxy->lms", ensemble, hits[1], preferred_element_type=jnp.float32
        )
        member_forcing = (picked * forcing[:, None]).astype(jnp.bfloat16)
    else:
        forcing = jnp.zeros((lev_dev, cell_count), jnp.float32)
        forcing = forcing.at[:, cell_index].add(arrived[:lev_dev].reshape(lev_dev, -1))
        forcing = forcing.reshape(lev_dev, col_count, row_count)
        member_forcing = (ensemble * forcing[:, None]).astype(jnp.bfloat16)

    regrouped = lax.all_to_all(member_forcing, "lev", split_axis=1, concat_axis=0, tiled=True)
    local_mix = jnp.einsum(
        "lk,lm...->km...", vert_root, regrouped, preferred_element_type=jnp.float32
    )
    level_mix = lax.all_to_all(
        local_mix.astype(jnp.bfloat16), "lev", split_axis=0, concat_axis=1, tiled=True
    )
    ends = tile_count - 1
    from_left = lax.ppermute(level_mix, "tile", [(i, i + 1) for i in range(ends)])
    from_right = lax.ppermute(level_mix, "tile", [(i + 1, i) for i in range(ends)])
    three = jnp.stack([from_left, level_mix, from_right])
    if packed:
        three = jnp.einsum(
            "tkms,tsxy->tkmxy", three, hits, preferred_element_type=jnp.float32
        ).astype(jnp.bfloat16)

    row_iota = jnp.arange(row_count, dtype=jnp.int32)
    taps_rows = taps_table(radius, row_iota[:, None] - row_iota[None, :])
    wide_iota = jnp.arange(3 * col_count, dtype=jnp.int32)
    col_iota = jnp.arange(col_count, dtype=jnp.int32)
    taps_cols = taps_table(radius, wide_iota[:, None] - col_count - col_iota[None, :])
    taps_cols = taps_cols.reshape(lev_dev, 3, col_count, col_count)
    smooth_wide = jnp.einsum(
        "tkmxy,kyz->tkmxz", three, taps_rows, preferred_element_type=jnp.float32
    ).astype(jnp.bfloat16)
    smooth_x = jnp.einsum(
        "tkmey,ktex->kmxy", smooth_wide, taps_cols, preferred_element_type=jnp.float32
    )
    gradient = alpha + smooth_x
    total_cells = float(lev_dev * group_count * col_count * tile_count * row_count)
    gram_local = (
        jnp.einsum("kmxy,knxy->mn", gradient, gradient, precision=lax.Precision.HIGHEST) / total_cells
    )
    gram_total = all_sum(gram_local, (("lev", group_count), ("tile", tile_count)))
    r_factor = jnp.linalg.cholesky(gram_total).T
    return (gradient, r_factor)


def solution(mesh):
    return jax.shard_map(
        shards,
        mesh=mesh,
        in_specs=(
            P("lev", "tile"),
            P("tile", None, None),
            P("tile", None, None),
            P("tile", None, None),
            P("tile", None),
            P("lev", None, "tile", None),
            P(),
            P("lev"),
            P("lev", None, "tile", None),
        ),
        out_specs=(P("lev", None, "tile", None), P()),
        check_vma=False,
    )
```

```python
import jax
import jax.numpy as jnp
from jax import lax
from jax.sharding import PartitionSpec as P

HALO = 16


def taps_table(radius, offsets):
    reach_max = radius.astype(jnp.float32)[:, None, None]
    distance = jnp.abs(offsets).astype(jnp.float32)[None]
    weights = jnp.where(
        distance <= reach_max, (reach_max + 1.0 - distance) / (reach_max + 1.0), 0.0
    )
    return weights.astype(jnp.bfloat16)


def first_hits(cells):
    slots = cells.shape[-1]
    same = cells[..., :, None] == cells[..., None, :]
    later = lax.broadcasted_iota(jnp.int32, (slots, slots), 1) < lax.broadcasted_iota(
        jnp.int32, (slots, slots), 0
    )
    return jnp.logical_not(jnp.any(same & later, axis=-1))


def one_hot(cells, keep, cell_count):
    grid = lax.broadcasted_iota(jnp.int32, cells.shape + (cell_count,), cells.ndim)
    hit = (cells[..., None] == grid) & keep[..., None]
    return hit.astype(jnp.bfloat16)


def all_sum(value, axes):
    if any(size & (size - 1) for _, size in axes):
        return lax.psum(value, tuple(name for name, _ in axes))
    for name, size in axes:
        bit = 1
        while bit < size:
            value = value + lax.ppermute(value, name, [(i, i ^ bit) for i in range(size)])
            bit *= 2
    return value


def shards(
    obs_adjoint, foot_obs, foot_cell, foot_weight, counts, ensemble, vert_root, radius, alpha
):
    lev_dev, members, col_count, row_count = alpha.shape
    tile_count = lax.axis_size("tile")
    group_count = lax.axis_size("lev")
    capacity = foot_obs.shape[2]
    cell_count = col_count * row_count
    slots = tile_count * capacity
    packed = slots < cell_count
    assert HALO <= col_count

    slot_index = lax.broadcasted_iota(jnp.int32, (tile_count, capacity), 1)
    live_mask = (slot_index < counts[0][:, None]).astype(jnp.float32)
    values = jnp.take(obs_adjoint, foot_obs[0], axis=1)
    payload = values * (foot_weight[0] * live_mask)[None]
    own_cells = foot_cell[0]
    prev_cells = jnp.concatenate([own_cells[:1], own_cells[:-1]], axis=0)
    next_cells = jnp.concatenate([own_cells[1:], own_cells[-1:]], axis=0)
    cell_rows = jnp.stack([prev_cells, own_cells, next_cells]).astype(jnp.float32)
    outgoing = jnp.concatenate([payload, cell_rows], axis=0)
    arrived = lax.all_to_all(outgoing, "tile", split_axis=1, concat_axis=1, tiled=True)
    near = arrived[lev_dev:].astype(jnp.int32).reshape(3, slots)
    cell_index = near[1]

    if packed:
        same = (cell_index[:, None] == cell_index[None, :]).astype(jnp.float32)
        forcing = jnp.einsum(
            "ls,st->lt", arrived[:lev_dev].reshape(lev_dev, -1), same,
            precision=lax.Precision.HIGHEST,
        )
        keep = first_hits(near)
        hits = one_hot(near, keep, cell_count).reshape(3, slots, col_count, row_count)
        picked = jnp.einsum(
            "lmxy,sxy->lms", ensemble, hits[1], preferred_element_type=jnp.float32
        )
        member_forcing = (picked * forcing[:, None]).astype(jnp.bfloat16)
    else:
        forcing = jnp.zeros((lev_dev, cell_count), jnp.float32)
        forcing = forcing.at[:, cell_index].add(arrived[:lev_dev].reshape(lev_dev, -1))
        forcing = forcing.reshape(lev_dev, col_count, row_count)
        member_forcing = (ensemble * forcing[:, None]).astype(jnp.bfloat16)

    regrouped = lax.all_to_all(member_forcing, "lev", split_axis=1, concat_axis=0, tiled=True)
    local_mix = jnp.einsum(
        "lk,lm...->km...", vert_root, regrouped, preferred_element_type=jnp.float32
    )
    level_mix = lax.all_to_all(
        local_mix.astype(jnp.bfloat16), "lev", split_axis=0, concat_axis=1, tiled=True
    )
    ends = tile_count - 1
    from_left = lax.ppermute(level_mix, "tile", [(i, i + 1) for i in range(ends)])
    from_right = lax.ppermute(level_mix, "tile", [(i + 1, i) for i in range(ends)])
    row_iota = jnp.arange(row_count, dtype=jnp.int32)
    taps_rows = taps_table(radius, row_iota[:, None] - row_iota[None, :])
    wide_iota = jnp.arange(3 * col_count, dtype=jnp.int32)
    col_iota = jnp.arange(col_count, dtype=jnp.int32)
    taps_cols = taps_table(radius, wide_iota[:, None] - col_count - col_iota[None, :])
    taps_cols = taps_cols.reshape(lev_dev, 3, col_count, col_count)

    def smoothed(mix, cells, side):
        if packed:
            mix = jnp.einsum(
                "kms,sxy->kmxy", mix, cells, preferred_element_type=jnp.float32
            ).astype(jnp.bfloat16)
        mix = jnp.einsum(
            "kmxy,kyz->kmxz", mix, taps_rows, preferred_element_type=jnp.float32
        ).astype(jnp.bfloat16)
        return jnp.einsum(
            "kmey,kex->kmxy", mix, taps_cols[:, side], preferred_element_type=jnp.float32
        )

    gradient = alpha + smoothed(level_mix, hits[1] if packed else None, 1)
    gradient = gradient + smoothed(from_left, hits[0] if packed else None, 0)
    gradient = gradient + smoothed(from_right, hits[2] if packed else None, 2)
    total_cells = float(lev_dev * group_count * col_count * tile_count * row_count)
    gram_local = (
        jnp.einsum("kmxy,knxy->mn", gradient, gradient, precision=lax.Precision.HIGH) / total_cells
    )
    gram_total = all_sum(gram_local, (("lev", group_count), ("tile", tile_count)))
    r_factor = jnp.linalg.cholesky(gram_total).T
    return (gradient, r_factor)


def solution(mesh):
    return jax.shard_map(
        shards,
        mesh=mesh,
        in_specs=(
            P("lev", "tile"),
            P("tile", None, None),
            P("tile", None, None),
            P("tile", None, None),
            P("tile", None),
            P("lev", None, "tile", None),
            P(),
            P("lev"),
            P("lev", None, "tile", None),
        ),
        out_specs=(P("lev", None, "tile", None), P()),
        check_vma=False,
    )
```

```python
import jax
import jax.numpy as jnp
from jax import lax
from jax.sharding import PartitionSpec as P

HALO = 16


def taps_table(radius, offsets):
    reach_max = radius.astype(jnp.float32)[:, None, None]
    distance = jnp.abs(offsets).astype(jnp.float32)[None]
    weights = jnp.where(
        distance <= reach_max, (reach_max + 1.0 - distance) / (reach_max + 1.0), 0.0
    )
    return weights.astype(jnp.bfloat16)


def first_hits(cells):
    slots = cells.shape[-1]
    same = cells[..., :, None] == cells[..., None, :]
    later = lax.broadcasted_iota(jnp.int32, (slots, slots), 1) < lax.broadcasted_iota(
        jnp.int32, (slots, slots), 0
    )
    return jnp.logical_not(jnp.any(same & later, axis=-1))


def one_hot(cells, keep, cell_count):
    grid = lax.broadcasted_iota(jnp.int32, cells.shape + (cell_count,), cells.ndim)
    hit = (cells[..., None] == grid) & keep[..., None]
    return hit.astype(jnp.bfloat16)


def all_sum(value, axes):
    for name, size in axes:
        if size == 1:
            continue
        if size > 8:
            bit = 1
            while bit < size and not size & (size - 1):
                value = value + lax.ppermute(value, name, [(i, i ^ bit) for i in range(size)])
                bit *= 2
            if size & (size - 1):
                value = lax.psum(value, name)
            continue
        got = [value] + [
            lax.ppermute(value, name, [(i, (i + shift) % size) for i in range(size)])
            for shift in range(1, size)
        ]
        here = lax.axis_index(name)
        order = (here - jnp.arange(size, dtype=jnp.int32)) % size
        parts = list(jnp.take(jnp.stack(got), order, axis=0))
        while len(parts) > 1:
            paired = [parts[i] + parts[i + 1] for i in range(0, len(parts) - 1, 2)]
            parts = paired + parts[len(parts) - len(parts) % 2:]
        value = parts[0]
    return value


def shards(
    obs_adjoint, foot_obs, foot_cell, foot_weight, counts, ensemble, vert_root, radius, alpha
):
    lev_dev, members, col_count, row_count = alpha.shape
    tile_count = lax.axis_size("tile")
    group_count = lax.axis_size("lev")
    capacity = foot_obs.shape[2]
    cell_count = col_count * row_count
    slots = tile_count * capacity
    packed = slots < cell_count
    assert HALO <= col_count

    slot_index = lax.broadcasted_iota(jnp.int32, (tile_count, capacity), 1)
    live_mask = (slot_index < counts[0][:, None]).astype(jnp.float32)
    values = jnp.take(obs_adjoint, foot_obs[0], axis=1)
    payload = values * (foot_weight[0] * live_mask)[None]
    own_cells = foot_cell[0]
    prev_cells = jnp.concatenate([own_cells[:1], own_cells[:-1]], axis=0)
    next_cells = jnp.concatenate([own_cells[1:], own_cells[-1:]], axis=0)
    cell_rows = jnp.stack([prev_cells, own_cells, next_cells]).astype(jnp.float32)
    outgoing = jnp.concatenate([payload, cell_rows], axis=0)
    arrived = lax.all_to_all(outgoing, "tile", split_axis=1, concat_axis=1, tiled=True)
    near = arrived[lev_dev:].astype(jnp.int32).reshape(3, slots)
    cell_index = near[1]

    if packed:
        same = (cell_index[:, None] == cell_index[None, :]).astype(jnp.float32)
        forcing = jnp.einsum(
            "ls,st->lt", arrived[:lev_dev].reshape(lev_dev, -1), same,
            precision=lax.Precision.HIGHEST,
        )
        keep = first_hits(near)
        hits = one_hot(near, keep, cell_count).reshape(3, slots, col_count, row_count)
        picked = jnp.einsum(
            "lmxy,sxy->lms", ensemble, hits[1], preferred_element_type=jnp.float32
        )
        member_forcing = (picked * forcing[:, None]).astype(jnp.bfloat16)
    else:
        forcing = jnp.zeros((lev_dev, cell_count), jnp.float32)
        forcing = forcing.at[:, cell_index].add(arrived[:lev_dev].reshape(lev_dev, -1))
        forcing = forcing.reshape(lev_dev, col_count, row_count)
        member_forcing = (ensemble * forcing[:, None]).astype(jnp.bfloat16)

    regrouped = lax.all_to_all(member_forcing, "lev", split_axis=1, concat_axis=0, tiled=True)
    local_mix = jnp.einsum(
        "lk,lm...->km...", vert_root, regrouped, preferred_element_type=jnp.float32
    )
    level_mix = lax.all_to_all(
        local_mix.astype(jnp.bfloat16), "lev", split_axis=0, concat_axis=1, tiled=True
    )
    ends = tile_count - 1
    from_left = lax.ppermute(level_mix, "tile", [(i, i + 1) for i in range(ends)])
    from_right = lax.ppermute(level_mix, "tile", [(i + 1, i) for i in range(ends)])
    three = jnp.stack([from_left, level_mix, from_right])
    if packed:
        three = jnp.einsum(
            "tkms,tsxy->tkmxy", three, hits, preferred_element_type=jnp.float32
        ).astype(jnp.bfloat16)

    row_iota = jnp.arange(row_count, dtype=jnp.int32)
    taps_rows = taps_table(radius, row_iota[:, None] - row_iota[None, :])
    wide_iota = jnp.arange(3 * col_count, dtype=jnp.int32)
    col_iota = jnp.arange(col_count, dtype=jnp.int32)
    taps_cols = taps_table(radius, wide_iota[:, None] - col_count - col_iota[None, :])
    taps_cols = taps_cols.reshape(lev_dev, 3, col_count, col_count)
    smooth_wide = jnp.einsum(
        "tkmxy,kyz->tkmxz", three, taps_rows, preferred_element_type=jnp.float32
    ).astype(jnp.bfloat16)
    smooth_x = jnp.einsum(
        "tkmey,ktex->kmxy", smooth_wide, taps_cols, preferred_element_type=jnp.float32
    )
    gradient = alpha + smooth_x
    total_cells = float(lev_dev * group_count * col_count * tile_count * row_count)
    gram_local = (
        jnp.einsum("kmxy,knxy->mn", gradient, gradient, precision=lax.Precision.HIGHEST) / total_cells
    )
    gram_total = all_sum(gram_local, (("lev", group_count), ("tile", tile_count)))
    r_factor = jnp.linalg.cholesky(gram_total).T
    return (gradient, r_factor)


def solution(mesh):
    return jax.shard_map(
        shards,
        mesh=mesh,
        in_specs=(
            P("lev", "tile"),
            P("tile", None, None),
            P("tile", None, None),
            P("tile", None, None),
            P("tile", None),
            P("lev", None, "tile", None),
            P(),
            P("lev"),
            P("lev", None, "tile", None),
        ),
        out_specs=(P("lev", None, "tile", None), P()),
        check_vma=False,
    )
```

```python
import jax
import jax.numpy as jnp
from jax import lax
from jax.sharding import PartitionSpec as P

HALO = 16


def taps_table(radius, offsets):
    reach_max = radius.astype(jnp.float32)[:, None, None]
    distance = jnp.abs(offsets).astype(jnp.float32)[None]
    weights = jnp.where(
        distance <= reach_max, (reach_max + 1.0 - distance) / (reach_max + 1.0), 0.0
    )
    return weights.astype(jnp.bfloat16)


def first_hits(cells):
    slots = cells.shape[-1]
    same = cells[..., :, None] == cells[..., None, :]
    later = lax.broadcasted_iota(jnp.int32, (slots, slots), 1) < lax.broadcasted_iota(
        jnp.int32, (slots, slots), 0
    )
    return jnp.logical_not(jnp.any(same & later, axis=-1))


def one_hot(cells, keep, cell_count):
    grid = lax.broadcasted_iota(jnp.int32, cells.shape + (cell_count,), cells.ndim)
    hit = (cells[..., None] == grid) & keep[..., None]
    return hit.astype(jnp.bfloat16)


def all_sum(value, axes):
    if any(size & (size - 1) for _, size in axes):
        return lax.psum(value, tuple(name for name, _ in axes))
    for name, size in axes:
        bit = 1
        while bit < size:
            value = value + lax.ppermute(value, name, [(i, i ^ bit) for i in range(size)])
            bit *= 2
    return value


def shards(
    obs_adjoint, foot_obs, foot_cell, foot_weight, counts, ensemble, vert_root, radius, alpha
):
    lev_dev, members, col_count, row_count = alpha.shape
    tile_count = lax.axis_size("tile")
    group_count = lax.axis_size("lev")
    capacity = foot_obs.shape[2]
    cell_count = col_count * row_count
    slots = tile_count * capacity
    packed = slots < cell_count
    assert HALO <= col_count

    slot_index = lax.broadcasted_iota(jnp.int32, (tile_count, capacity), 1)
    live_mask = (slot_index < counts[0][:, None]).astype(jnp.float32)
    values = jnp.take(obs_adjoint, foot_obs[0], axis=1)
    payload = values * (foot_weight[0] * live_mask)[None]
    own_cells = foot_cell[0]
    prev_cells = jnp.concatenate([own_cells[:1], own_cells[:-1]], axis=0)
    next_cells = jnp.concatenate([own_cells[1:], own_cells[-1:]], axis=0)
    cell_rows = jnp.stack([prev_cells, own_cells, next_cells]).astype(jnp.float32)
    outgoing = jnp.concatenate([payload, cell_rows], axis=0)
    arrived = lax.all_to_all(outgoing, "tile", split_axis=1, concat_axis=1, tiled=True)
    near = arrived[lev_dev:].astype(jnp.int32).reshape(3, slots)
    cell_index = near[1]

    if packed:
        same = (cell_index[:, None] == cell_index[None, :]).astype(jnp.float32)
        forcing = jnp.einsum(
            "ls,st->lt", arrived[:lev_dev].reshape(lev_dev, -1), same,
            precision=lax.Precision.HIGHEST,
        )
        own_keep = first_hits(cell_index)

        def own_hits():
            return one_hot(cell_index, own_keep, cell_count).reshape(slots, col_count, row_count)

        picked = jnp.einsum(
            "lmxy,sxy->lms", ensemble, own_hits(), preferred_element_type=jnp.float32
        )
        member_forcing = (picked * forcing[:, None]).astype(jnp.bfloat16)
    else:
        forcing = jnp.zeros((lev_dev, cell_count), jnp.float32)
        forcing = forcing.at[:, cell_index].add(arrived[:lev_dev].reshape(lev_dev, -1))
        forcing = forcing.reshape(lev_dev, col_count, row_count)
        member_forcing = (ensemble * forcing[:, None]).astype(jnp.bfloat16)

    regrouped = lax.all_to_all(member_forcing, "lev", split_axis=1, concat_axis=0, tiled=True)
    local_mix = jnp.einsum(
        "lk,lm...->km...", vert_root, regrouped, preferred_element_type=jnp.float32
    )
    level_mix = lax.all_to_all(
        local_mix.astype(jnp.bfloat16), "lev", split_axis=0, concat_axis=1, tiled=True
    )
    ends = tile_count - 1
    from_left = lax.ppermute(level_mix, "tile", [(i, i + 1) for i in range(ends)])
    from_right = lax.ppermute(level_mix, "tile", [(i + 1, i) for i in range(ends)])
    row_iota = jnp.arange(row_count, dtype=jnp.int32)
    taps_rows = taps_table(radius, row_iota[:, None] - row_iota[None, :])
    wide_iota = jnp.arange(3 * col_count, dtype=jnp.int32)
    col_iota = jnp.arange(col_count, dtype=jnp.int32)
    taps_cols = taps_table(radius, wide_iota[:, None] - col_count - col_iota[None, :])
    taps_cols = taps_cols.reshape(lev_dev, 3, col_count, col_count)

    own = level_mix
    if packed:
        own = jnp.einsum(
            "kms,sxy->kmxy", own, own_hits(), preferred_element_type=jnp.float32
        ).astype(jnp.bfloat16)
    own = jnp.einsum(
        "kmxy,kyz->kmxz", own, taps_rows, preferred_element_type=jnp.float32
    ).astype(jnp.bfloat16)
    own = jnp.einsum(
        "kmey,kex->kmxy", own, taps_cols[:, 1], preferred_element_type=jnp.float32
    )
    gradient = alpha + own

    sides = jnp.stack([from_left, from_right])
    if packed:
        side_cells = near[0::2]
        side_hits = one_hot(side_cells, first_hits(side_cells), cell_count)
        sides = jnp.einsum(
            "tkms,tsxy->tkmxy", sides,
            side_hits.reshape(2, slots, col_count, row_count),
            preferred_element_type=jnp.float32,
        ).astype(jnp.bfloat16)
    sides = jnp.einsum(
        "tkmxy,kyz->tkmxz", sides, taps_rows, preferred_element_type=jnp.float32
    ).astype(jnp.bfloat16)
    smooth_x = jnp.einsum(
        "tkmey,ktex->kmxy", sides, taps_cols[:, 0::2], preferred_element_type=jnp.float32
    )
    gradient = gradient + smooth_x
    total_cells = float(lev_dev * group_count * col_count * tile_count * row_count)
    gram_local = (
        jnp.einsum("kmxy,knxy->mn", gradient, gradient, precision=lax.Precision.HIGHEST) / total_cells
    )
    gram_total = all_sum(gram_local, (("lev", group_count), ("tile", tile_count)))
    r_factor = jnp.linalg.cholesky(gram_total).T
    return (gradient, r_factor)


def solution(mesh):
    return jax.shard_map(
        shards,
        mesh=mesh,
        in_specs=(
            P("lev", "tile"),
            P("tile", None, None),
            P("tile", None, None),
            P("tile", None, None),
            P("tile", None),
            P("lev", None, "tile", None),
            P(),
            P("lev"),
            P("lev", None, "tile", None),
        ),
        out_specs=(P("lev", None, "tile", None), P()),
        check_vma=False,
    )
```

```python
import jax
import jax.numpy as jnp
from jax import lax
from jax.sharding import PartitionSpec as P

HALO = 16


def taps_table(radius, offsets):
    reach_max = radius.astype(jnp.float32)[:, None, None]
    distance = jnp.abs(offsets).astype(jnp.float32)[None]
    weights = jnp.where(
        distance <= reach_max, (reach_max + 1.0 - distance) / (reach_max + 1.0), 0.0
    )
    return weights.astype(jnp.bfloat16)


def first_hits(cells):
    slots = cells.shape[-1]
    same = cells[..., :, None] == cells[..., None, :]
    later = lax.broadcasted_iota(jnp.int32, (slots, slots), 1) < lax.broadcasted_iota(
        jnp.int32, (slots, slots), 0
    )
    return jnp.logical_not(jnp.any(same & later, axis=-1))


def one_hot(cells, keep, cell_count):
    grid = lax.broadcasted_iota(jnp.int32, cells.shape + (cell_count,), cells.ndim)
    hit = (cells[..., None] == grid) & keep[..., None]
    return hit.astype(jnp.bfloat16)


def all_sum(value, axes):
    if any(size & (size - 1) for _, size in axes):
        return lax.psum(value, tuple(name for name, _ in axes))
    for name, size in axes:
        bit = 1
        while bit < size:
            value = value + lax.ppermute(value, name, [(i, i ^ bit) for i in range(size)])
            bit *= 2
    return value


def gram_of(panel):
    high = panel.astype(jnp.bfloat16)
    low = (panel - high.astype(jnp.float32)).astype(jnp.bfloat16)
    members = panel.shape[1]
    parts = jnp.concatenate([high, low], axis=1)
    blocks = jnp.einsum("kpxy,kqxy->pq", parts, parts, preferred_element_type=jnp.float32)
    top, bottom = blocks[:members], blocks[members:]
    return (top[:, :members] + top[:, members:]) + (bottom[:, :members] + bottom[:, members:])


def shards(
    obs_adjoint, foot_obs, foot_cell, foot_weight, counts, ensemble, vert_root, radius, alpha
):
    lev_dev, members, col_count, row_count = alpha.shape
    tile_count = lax.axis_size("tile")
    group_count = lax.axis_size("lev")
    capacity = foot_obs.shape[2]
    cell_count = col_count * row_count
    slots = tile_count * capacity
    packed = slots < cell_count
    assert HALO <= col_count

    slot_index = lax.broadcasted_iota(jnp.int32, (tile_count, capacity), 1)
    live_mask = (slot_index < counts[0][:, None]).astype(jnp.float32)
    values = jnp.take(obs_adjoint, foot_obs[0], axis=1)
    payload = values * (foot_weight[0] * live_mask)[None]
    own_cells = foot_cell[0]
    prev_cells = jnp.concatenate([own_cells[:1], own_cells[:-1]], axis=0)
    next_cells = jnp.concatenate([own_cells[1:], own_cells[-1:]], axis=0)
    cell_rows = jnp.stack([prev_cells, own_cells, next_cells]).astype(jnp.float32)
    outgoing = jnp.concatenate([payload, cell_rows], axis=0)
    arrived = lax.all_to_all(outgoing, "tile", split_axis=1, concat_axis=1, tiled=True)
    near = arrived[lev_dev:].astype(jnp.int32).reshape(3, slots)
    cell_index = near[1]

    if packed:
        same = (cell_index[:, None] == cell_index[None, :]).astype(jnp.float32)
        forcing = jnp.einsum(
            "ls,st->lt", arrived[:lev_dev].reshape(lev_dev, -1), same,
            precision=lax.Precision.HIGHEST,
        )
        own_keep = first_hits(cell_index)

        def own_hits():
            return one_hot(cell_index, own_keep, cell_count).reshape(slots, col_count, row_count)

        picked = jnp.einsum(
            "lmxy,sxy->lms", ensemble, own_hits(), preferred_element_type=jnp.float32
        )
        member_forcing = (picked * forcing[:, None]).astype(jnp.bfloat16)
    else:
        forcing = jnp.zeros((lev_dev, cell_count), jnp.float32)
        forcing = forcing.at[:, cell_index].add(arrived[:lev_dev].reshape(lev_dev, -1))
        forcing = forcing.reshape(lev_dev, col_count, row_count)
        member_forcing = (ensemble * forcing[:, None]).astype(jnp.bfloat16)

    regrouped = lax.all_to_all(member_forcing, "lev", split_axis=1, concat_axis=0, tiled=True)
    local_mix = jnp.einsum(
        "lk,lm...->km...", vert_root, regrouped, preferred_element_type=jnp.float32
    )
    level_mix = lax.all_to_all(
        local_mix.astype(jnp.bfloat16), "lev", split_axis=0, concat_axis=1, tiled=True
    )
    ends = tile_count - 1
    from_left = lax.ppermute(level_mix, "tile", [(i, i + 1) for i in range(ends)])
    from_right = lax.ppermute(level_mix, "tile", [(i + 1, i) for i in range(ends)])
    row_iota = jnp.arange(row_count, dtype=jnp.int32)
    taps_rows = taps_table(radius, row_iota[:, None] - row_iota[None, :])
    wide_iota = jnp.arange(3 * col_count, dtype=jnp.int32)
    col_iota = jnp.arange(col_count, dtype=jnp.int32)
    taps_cols = taps_table(radius, wide_iota[:, None] - col_count - col_iota[None, :])
    taps_cols = taps_cols.reshape(lev_dev, 3, col_count, col_count)

    own = level_mix
    if packed:
        own = jnp.einsum(
            "kms,sxy->kmxy", own, own_hits(), preferred_element_type=jnp.float32
        ).astype(jnp.bfloat16)
    own = jnp.einsum(
        "kmxy,kyz->kmxz", own, taps_rows, preferred_element_type=jnp.float32
    ).astype(jnp.bfloat16)
    own = jnp.einsum(
        "kmey,kex->kmxy", own, taps_cols[:, 1], preferred_element_type=jnp.float32
    )
    gradient = alpha + own

    sides = jnp.stack([from_left, from_right])
    if packed:
        side_cells = near[0::2]
        side_hits = one_hot(side_cells, first_hits(side_cells), cell_count)
        sides = jnp.einsum(
            "tkms,tsxy->tkmxy", sides,
            side_hits.reshape(2, slots, col_count, row_count),
            preferred_element_type=jnp.float32,
        ).astype(jnp.bfloat16)
    sides = jnp.einsum(
        "tkmxy,kyz->tkmxz", sides, taps_rows, preferred_element_type=jnp.float32
    ).astype(jnp.bfloat16)
    smooth_x = jnp.einsum(
        "tkmey,ktex->kmxy", sides, taps_cols[:, 0::2], preferred_element_type=jnp.float32
    )
    gradient = gradient + smooth_x
    total_cells = float(lev_dev * group_count * col_count * tile_count * row_count)
    gram_local = (
        gram_of(gradient) / total_cells
    )
    gram_total = all_sum(gram_local, (("lev", group_count), ("tile", tile_count)))
    r_factor = jnp.linalg.cholesky(gram_total).T
    return (gradient, r_factor)


def solution(mesh):
    return jax.shard_map(
        shards,
        mesh=mesh,
        in_specs=(
            P("lev", "tile"),
            P("tile", None, None),
            P("tile", None, None),
            P("tile", None, None),
            P("tile", None),
            P("lev", None, "tile", None),
            P(),
            P("lev"),
            P("lev", None, "tile", None),
        ),
        out_specs=(P("lev", None, "tile", None), P()),
        check_vma=False,
    )
```

```python
import jax
import jax.numpy as jnp
from jax import lax
from jax.sharding import PartitionSpec as P

HALO = 16


def taps_table(radius, offsets):
    reach_max = radius.astype(jnp.float32)[:, None, None]
    distance = jnp.abs(offsets).astype(jnp.float32)[None]
    weights = jnp.where(
        distance <= reach_max, (reach_max + 1.0 - distance) / (reach_max + 1.0), 0.0
    )
    return weights.astype(jnp.bfloat16)


def first_hits(cells):
    slots = cells.shape[-1]
    same = cells[..., :, None] == cells[..., None, :]
    later = lax.broadcasted_iota(jnp.int32, (slots, slots), 1) < lax.broadcasted_iota(
        jnp.int32, (slots, slots), 0
    )
    return jnp.logical_not(jnp.any(same & later, axis=-1))


def one_hot(cells, keep, cell_count):
    grid = lax.broadcasted_iota(jnp.int32, cells.shape + (cell_count,), cells.ndim)
    hit = (cells[..., None] == grid) & keep[..., None]
    return hit.astype(jnp.bfloat16)


def all_sum(value, axes):
    if any(size & (size - 1) for _, size in axes):
        return lax.psum(value, tuple(name for name, _ in axes))
    for name, size in axes:
        bit = 1
        while bit < size:
            value = value + lax.ppermute(value, name, [(i, i ^ bit) for i in range(size)])
            bit *= 2
    return value


def spread(mix, cells, keep, taps_rows, col_count, row_count):
    rows = cells % row_count
    cols = cells // row_count
    row_hit = (rows[:, None] == jnp.arange(row_count, dtype=jnp.int32)[None, :]) & keep[:, None]
    slot_taps = jnp.einsum(
        "sy,kyz->ksz", row_hit.astype(jnp.bfloat16), taps_rows,
        preferred_element_type=jnp.float32,
    ).astype(jnp.bfloat16)
    col_hit = cols[:, None] == jnp.arange(col_count, dtype=jnp.int32)[None, :]
    weights = jnp.where(col_hit[None, :, :, None], slot_taps[:, :, None, :], 0).astype(jnp.bfloat16)
    return jnp.einsum(
        "kms,ksxz->kmxz", mix, weights, preferred_element_type=jnp.float32
    ).astype(jnp.bfloat16)


def gram_of(panel):
    high = panel.astype(jnp.bfloat16)
    low = (panel - high.astype(jnp.float32)).astype(jnp.bfloat16)
    members = panel.shape[1]
    parts = jnp.concatenate([high, low], axis=1)
    blocks = jnp.einsum("kpxy,kqxy->pq", parts, parts, preferred_element_type=jnp.float32)
    top, bottom = blocks[:members], blocks[members:]
    return (top[:, :members] + top[:, members:]) + (bottom[:, :members] + bottom[:, members:])


def shards(
    obs_adjoint, foot_obs, foot_cell, foot_weight, counts, ensemble, vert_root, radius, alpha
):
    lev_dev, members, col_count, row_count = alpha.shape
    tile_count = lax.axis_size("tile")
    group_count = lax.axis_size("lev")
    capacity = foot_obs.shape[2]
    cell_count = col_count * row_count
    slots = tile_count * capacity
    packed = slots < cell_count
    assert HALO <= col_count

    slot_index = lax.broadcasted_iota(jnp.int32, (tile_count, capacity), 1)
    live_mask = (slot_index < counts[0][:, None]).astype(jnp.float32)
    values = jnp.take(obs_adjoint, foot_obs[0], axis=1)
    payload = values * (foot_weight[0] * live_mask)[None]
    own_cells = foot_cell[0]
    prev_cells = jnp.concatenate([own_cells[:1], own_cells[:-1]], axis=0)
    next_cells = jnp.concatenate([own_cells[1:], own_cells[-1:]], axis=0)
    cell_rows = jnp.stack([prev_cells, own_cells, next_cells]).astype(jnp.float32)
    outgoing = jnp.concatenate([payload, cell_rows], axis=0)
    arrived = lax.all_to_all(outgoing, "tile", split_axis=1, concat_axis=1, tiled=True)
    near = arrived[lev_dev:].astype(jnp.int32).reshape(3, slots)
    cell_index = near[1]

    if packed:
        same = (cell_index[:, None] == cell_index[None, :]).astype(jnp.float32)
        forcing = jnp.einsum(
            "ls,st->lt", arrived[:lev_dev].reshape(lev_dev, -1), same,
            precision=lax.Precision.HIGHEST,
        )
        own_keep = first_hits(cell_index)

        def own_hits():
            return one_hot(cell_index, own_keep, cell_count).reshape(slots, col_count, row_count)

        picked = jnp.einsum(
            "lmxy,sxy->lms", ensemble, own_hits(), preferred_element_type=jnp.float32
        )
        member_forcing = (picked * forcing[:, None]).astype(jnp.bfloat16)
    else:
        forcing = jnp.zeros((lev_dev, cell_count), jnp.float32)
        forcing = forcing.at[:, cell_index].add(arrived[:lev_dev].reshape(lev_dev, -1))
        forcing = forcing.reshape(lev_dev, col_count, row_count)
        member_forcing = (ensemble * forcing[:, None]).astype(jnp.bfloat16)

    regrouped = lax.all_to_all(member_forcing, "lev", split_axis=1, concat_axis=0, tiled=True)
    local_mix = jnp.einsum(
        "lk,lm...->km...", vert_root, regrouped, preferred_element_type=jnp.float32
    )
    level_mix = lax.all_to_all(
        local_mix.astype(jnp.bfloat16), "lev", split_axis=0, concat_axis=1, tiled=True
    )
    ends = tile_count - 1
    from_left = lax.ppermute(level_mix, "tile", [(i, i + 1) for i in range(ends)])
    from_right = lax.ppermute(level_mix, "tile", [(i + 1, i) for i in range(ends)])
    row_iota = jnp.arange(row_count, dtype=jnp.int32)
    taps_rows = taps_table(radius, row_iota[:, None] - row_iota[None, :])
    wide_iota = jnp.arange(3 * col_count, dtype=jnp.int32)
    col_iota = jnp.arange(col_count, dtype=jnp.int32)
    taps_cols = taps_table(radius, wide_iota[:, None] - col_count - col_iota[None, :])
    taps_cols = taps_cols.reshape(lev_dev, 3, col_count, col_count)

    if packed:
        own = spread(level_mix, cell_index, own_keep, taps_rows, col_count, row_count)
    else:
        own = jnp.einsum(
            "kmxy,kyz->kmxz", level_mix, taps_rows, preferred_element_type=jnp.float32
        ).astype(jnp.bfloat16)
    own = jnp.einsum(
        "kmey,kex->kmxy", own, taps_cols[:, 1], preferred_element_type=jnp.float32
    )
    gradient = alpha + own

    sides = jnp.stack([from_left, from_right])
    if packed:
        side_cells = near[0::2]
        sides = jax.vmap(spread, in_axes=(0, 0, 0, None, None, None))(
            sides, side_cells, first_hits(side_cells), taps_rows, col_count, row_count
        )
    else:
        sides = jnp.einsum(
            "tkmxy,kyz->tkmxz", sides, taps_rows, preferred_element_type=jnp.float32
        ).astype(jnp.bfloat16)
    smooth_x = jnp.einsum(
        "tkmey,ktex->kmxy", sides, taps_cols[:, 0::2], preferred_element_type=jnp.float32
    )
    gradient = gradient + smooth_x
    total_cells = float(lev_dev * group_count * col_count * tile_count * row_count)
    gram_local = (
        gram_of(gradient) / total_cells
    )
    gram_total = all_sum(gram_local, (("lev", group_count), ("tile", tile_count)))
    r_factor = jnp.linalg.cholesky(gram_total).T
    return (gradient, r_factor)


def solution(mesh):
    return jax.shard_map(
        shards,
        mesh=mesh,
        in_specs=(
            P("lev", "tile"),
            P("tile", None, None),
            P("tile", None, None),
            P("tile", None, None),
            P("tile", None),
            P("lev", None, "tile", None),
            P(),
            P("lev"),
            P("lev", None, "tile", None),
        ),
        out_specs=(P("lev", None, "tile", None), P()),
        check_vma=False,
    )
```

```python
import jax
import jax.numpy as jnp
from jax import lax
from jax.sharding import PartitionSpec as P

HALO = 16


def taps_table(radius, offsets):
    reach_max = radius.astype(jnp.float32)[:, None, None]
    distance = jnp.abs(offsets).astype(jnp.float32)[None]
    weights = jnp.where(
        distance <= reach_max, (reach_max + 1.0 - distance) / (reach_max + 1.0), 0.0
    )
    return weights.astype(jnp.bfloat16)


def first_hits(cells):
    slots = cells.shape[-1]
    same = cells[..., :, None] == cells[..., None, :]
    later = lax.broadcasted_iota(jnp.int32, (slots, slots), 1) < lax.broadcasted_iota(
        jnp.int32, (slots, slots), 0
    )
    return jnp.logical_not(jnp.any(same & later, axis=-1))


def one_hot(cells, keep, cell_count):
    grid = lax.broadcasted_iota(jnp.int32, cells.shape + (cell_count,), cells.ndim)
    hit = (cells[..., None] == grid) & keep[..., None]
    return hit.astype(jnp.bfloat16)


def all_sum(value, axes):
    if any(size & (size - 1) for _, size in axes):
        return lax.psum(value, tuple(name for name, _ in axes))
    for name, size in axes:
        bit = 1
        while bit < size:
            value = value + lax.ppermute(value, name, [(i, i ^ bit) for i in range(size)])
            bit *= 2
    return value


def spread(mix, cells, keep, radius, col_count, row_count):
    rows = cells % row_count
    cols = cells // row_count
    offsets = rows[:, None] - jnp.arange(row_count, dtype=jnp.int32)[None, :]
    slot_taps = taps_table(radius, offsets) * keep[None, :, None].astype(jnp.bfloat16)
    col_hit = cols[None, :] == jnp.arange(col_count, dtype=jnp.int32)[:, None]
    placed = jnp.where(col_hit[None, None], mix[:, :, None, :], 0).astype(jnp.bfloat16)
    return jnp.einsum(
        "kmxs,ksz->kmxz", placed, slot_taps, preferred_element_type=jnp.float32
    ).astype(jnp.bfloat16)


def gram_of(panel):
    high = panel.astype(jnp.bfloat16)
    low = (panel - high.astype(jnp.float32)).astype(jnp.bfloat16)
    members = panel.shape[1]
    parts = jnp.concatenate([high, low], axis=1)
    blocks = jnp.einsum("kpxy,kqxy->pq", parts, parts, preferred_element_type=jnp.float32)
    top, bottom = blocks[:members], blocks[members:]
    return (top[:, :members] + top[:, members:]) + (bottom[:, :members] + bottom[:, members:])


def shards(
    obs_adjoint, foot_obs, foot_cell, foot_weight, counts, ensemble, vert_root, radius, alpha
):
    lev_dev, members, col_count, row_count = alpha.shape
    tile_count = lax.axis_size("tile")
    group_count = lax.axis_size("lev")
    capacity = foot_obs.shape[2]
    cell_count = col_count * row_count
    slots = tile_count * capacity
    packed = slots < cell_count
    assert HALO <= col_count

    slot_index = lax.broadcasted_iota(jnp.int32, (tile_count, capacity), 1)
    live_mask = (slot_index < counts[0][:, None]).astype(jnp.float32)
    values = jnp.take(obs_adjoint, foot_obs[0], axis=1)
    payload = values * (foot_weight[0] * live_mask)[None]
    own_cells = foot_cell[0]
    prev_cells = jnp.concatenate([own_cells[:1], own_cells[:-1]], axis=0)
    next_cells = jnp.concatenate([own_cells[1:], own_cells[-1:]], axis=0)
    cell_rows = jnp.stack([prev_cells, own_cells, next_cells]).astype(jnp.float32)
    outgoing = jnp.concatenate([payload, cell_rows], axis=0)
    arrived = lax.all_to_all(outgoing, "tile", split_axis=1, concat_axis=1, tiled=True)
    near = arrived[lev_dev:].astype(jnp.int32).reshape(3, slots)
    cell_index = near[1]

    if packed:
        same = (cell_index[:, None] == cell_index[None, :]).astype(jnp.float32)
        forcing = jnp.einsum(
            "ls,st->lt", arrived[:lev_dev].reshape(lev_dev, -1), same,
            precision=lax.Precision.HIGHEST,
        )
        own_keep = first_hits(cell_index)

        def own_hits():
            return one_hot(cell_index, own_keep, cell_count).reshape(slots, col_count, row_count)

        picked = jnp.einsum(
            "lmxy,sxy->lms", ensemble, own_hits(), preferred_element_type=jnp.float32
        )
        member_forcing = (picked * forcing[:, None]).astype(jnp.bfloat16)
    else:
        forcing = jnp.zeros((lev_dev, cell_count), jnp.float32)
        forcing = forcing.at[:, cell_index].add(arrived[:lev_dev].reshape(lev_dev, -1))
        forcing = forcing.reshape(lev_dev, col_count, row_count)
        member_forcing = (ensemble * forcing[:, None]).astype(jnp.bfloat16)

    regrouped = lax.all_to_all(member_forcing, "lev", split_axis=1, concat_axis=0, tiled=True)
    local_mix = jnp.einsum(
        "lk,lm...->km...", vert_root, regrouped, preferred_element_type=jnp.float32
    )
    level_mix = lax.all_to_all(
        local_mix.astype(jnp.bfloat16), "lev", split_axis=0, concat_axis=1, tiled=True
    )
    ends = tile_count - 1
    from_left = lax.ppermute(level_mix, "tile", [(i, i + 1) for i in range(ends)])
    from_right = lax.ppermute(level_mix, "tile", [(i + 1, i) for i in range(ends)])
    row_iota = jnp.arange(row_count, dtype=jnp.int32)
    taps_rows = taps_table(radius, row_iota[:, None] - row_iota[None, :])
    wide_iota = jnp.arange(3 * col_count, dtype=jnp.int32)
    col_iota = jnp.arange(col_count, dtype=jnp.int32)
    taps_cols = taps_table(radius, wide_iota[:, None] - col_count - col_iota[None, :])
    taps_cols = taps_cols.reshape(lev_dev, 3, col_count, col_count)

    if packed:
        own = spread(level_mix, cell_index, own_keep, radius, col_count, row_count)
    else:
        own = jnp.einsum(
            "kmxy,kyz->kmxz", level_mix, taps_rows, preferred_element_type=jnp.float32
        ).astype(jnp.bfloat16)
    own = jnp.einsum(
        "kmey,kex->kmxy", own, taps_cols[:, 1], preferred_element_type=jnp.float32
    )
    gradient = alpha + own

    sides = jnp.stack([from_left, from_right])
    if packed:
        side_cells = near[0::2]
        sides = jax.vmap(spread, in_axes=(0, 0, 0, None, None, None))(
            sides, side_cells, first_hits(side_cells), radius, col_count, row_count
        )
    else:
        sides = jnp.einsum(
            "tkmxy,kyz->tkmxz", sides, taps_rows, preferred_element_type=jnp.float32
        ).astype(jnp.bfloat16)
    smooth_x = jnp.einsum(
        "tkmey,ktex->kmxy", sides, taps_cols[:, 0::2], preferred_element_type=jnp.float32
    )
    gradient = gradient + smooth_x
    total_cells = float(lev_dev * group_count * col_count * tile_count * row_count)
    gram_local = (
        gram_of(gradient) / total_cells
    )
    gram_total = all_sum(gram_local, (("lev", group_count), ("tile", tile_count)))
    r_factor = jnp.linalg.cholesky(gram_total).T
    return (gradient, r_factor)


def solution(mesh):
    return jax.shard_map(
        shards,
        mesh=mesh,
        in_specs=(
            P("lev", "tile"),
            P("tile", None, None),
            P("tile", None, None),
            P("tile", None, None),
            P("tile", None),
            P("lev", None, "tile", None),
            P(),
            P("lev"),
            P("lev", None, "tile", None),
        ),
        out_specs=(P("lev", None, "tile", None), P()),
        check_vma=False,
    )
```

```python
import jax
import jax.numpy as jnp
from jax import lax
from jax.sharding import PartitionSpec as P

HALO = 16


def taps_table(radius, offsets):
    reach_max = radius.astype(jnp.float32)[:, None, None]
    distance = jnp.abs(offsets).astype(jnp.float32)[None]
    weights = jnp.where(
        distance <= reach_max, (reach_max + 1.0 - distance) / (reach_max + 1.0), 0.0
    )
    return weights.astype(jnp.bfloat16)


def first_hits(cells):
    slots = cells.shape[-1]
    same = cells[..., :, None] == cells[..., None, :]
    later = lax.broadcasted_iota(jnp.int32, (slots, slots), 1) < lax.broadcasted_iota(
        jnp.int32, (slots, slots), 0
    )
    return jnp.logical_not(jnp.any(same & later, axis=-1))


def one_hot(cells, keep, cell_count):
    grid = lax.broadcasted_iota(jnp.int32, cells.shape + (cell_count,), cells.ndim)
    hit = (cells[..., None] == grid) & keep[..., None]
    return hit.astype(jnp.bfloat16)


def all_sum(value, axes):
    if any(size & (size - 1) for _, size in axes):
        return lax.psum(value, tuple(name for name, _ in axes))
    for name, size in axes:
        bit = 1
        while bit < size:
            value = value + lax.ppermute(value, name, [(i, i ^ bit) for i in range(size)])
            bit *= 2
    return value


def spread(mix, cells, keep, radius, col_count, row_count):
    rows = cells % row_count
    cols = cells // row_count
    offsets = rows[:, None] - jnp.arange(row_count, dtype=jnp.int32)[None, :]
    slot_taps = taps_table(radius, offsets) * keep[None, :, None].astype(jnp.bfloat16)
    col_hit = cols[None, :] == jnp.arange(col_count, dtype=jnp.int32)[:, None]
    placed = jnp.where(col_hit[None, None, None], mix[:, :, :, None, :], 0).astype(jnp.bfloat16)
    out = jnp.einsum(
        "gkmxs,ksz->kgmxz", placed, slot_taps, preferred_element_type=jnp.float32
    ).astype(jnp.bfloat16)
    return out.reshape((out.shape[0], -1) + out.shape[3:])


def gram_of(panel):
    high = panel.astype(jnp.bfloat16)
    low = (panel - high.astype(jnp.float32)).astype(jnp.bfloat16)
    members = panel.shape[1]
    parts = jnp.concatenate([high, low], axis=1)
    blocks = jnp.einsum("kpxy,kqxy->pq", parts, parts, preferred_element_type=jnp.float32)
    top, bottom = blocks[:members], blocks[members:]
    return (top[:, :members] + top[:, members:]) + (bottom[:, :members] + bottom[:, members:])


def shards(
    obs_adjoint, foot_obs, foot_cell, foot_weight, counts, ensemble, vert_root, radius, alpha
):
    lev_dev, members, col_count, row_count = alpha.shape
    tile_count = lax.axis_size("tile")
    group_count = lax.axis_size("lev")
    capacity = foot_obs.shape[2]
    cell_count = col_count * row_count
    slots = tile_count * capacity
    packed = slots < cell_count
    share = members // group_count
    assert HALO <= col_count

    slot_index = lax.broadcasted_iota(jnp.int32, (tile_count, capacity), 1)
    live_mask = (slot_index < counts[0][:, None]).astype(jnp.float32)
    obs_hit = foot_obs[0][:, :, None] == lax.broadcasted_iota(
        jnp.int32, (1, 1, obs_adjoint.shape[1]), 2
    )
    values = jnp.einsum(
        "lo,dco->ldc", obs_adjoint, obs_hit.astype(jnp.float32),
        precision=lax.Precision.HIGHEST,
    )
    payload = values * (foot_weight[0] * live_mask)[None]
    own_cells = foot_cell[0]
    prev_cells = jnp.concatenate([own_cells[:1], own_cells[:-1]], axis=0)
    next_cells = jnp.concatenate([own_cells[1:], own_cells[-1:]], axis=0)
    cell_rows = jnp.stack([prev_cells, own_cells, next_cells]).astype(jnp.float32)
    outgoing = jnp.concatenate([payload, cell_rows], axis=0)
    arrived = lax.all_to_all(outgoing, "tile", split_axis=1, concat_axis=1, tiled=True)
    near = arrived[lev_dev:].astype(jnp.int32).reshape(3, slots)
    cell_index = near[1]

    if packed:
        same = (cell_index[:, None] == cell_index[None, :]).astype(jnp.float32)
        forcing = jnp.einsum(
            "ls,st->lt", arrived[:lev_dev].reshape(lev_dev, -1), same,
            precision=lax.Precision.HIGHEST,
        )
        own_keep = first_hits(cell_index)

        def own_hits():
            return one_hot(cell_index, own_keep, cell_count).reshape(slots, col_count, row_count)

        picked = jnp.einsum(
            "lgmxy,sxy->glms", ensemble.reshape(lev_dev, group_count, share, col_count, row_count),
            own_hits(), preferred_element_type=jnp.float32,
        )
        member_forcing = (picked * forcing[None, :, None]).astype(jnp.bfloat16)
    else:
        forcing = jnp.zeros((lev_dev, cell_count), jnp.float32)
        forcing = forcing.at[:, cell_index].add(arrived[:lev_dev].reshape(lev_dev, -1))
        forcing = forcing.reshape(lev_dev, col_count, row_count)
        member_forcing = (ensemble * forcing[:, None]).astype(jnp.bfloat16)
        member_forcing = jnp.swapaxes(
            member_forcing.reshape((lev_dev, group_count, share) + member_forcing.shape[2:]), 0, 1
        )

    regrouped = lax.all_to_all(member_forcing, "lev", split_axis=0, concat_axis=0, tiled=True)
    regrouped = regrouped.reshape((group_count * lev_dev,) + regrouped.shape[2:])
    local_mix = jnp.einsum(
        "lk,lm...->km...", vert_root, regrouped, preferred_element_type=jnp.float32
    ).astype(jnp.bfloat16)
    local_mix = local_mix.reshape((group_count, lev_dev) + local_mix.shape[1:])
    level_mix = lax.all_to_all(local_mix, "lev", split_axis=0, concat_axis=0, tiled=True)
    if not packed:
        level_mix = jnp.swapaxes(level_mix, 0, 1).reshape(
            (lev_dev, members) + level_mix.shape[3:]
        )
    ends = tile_count - 1
    from_left = lax.ppermute(level_mix, "tile", [(i, i + 1) for i in range(ends)])
    from_right = lax.ppermute(level_mix, "tile", [(i + 1, i) for i in range(ends)])
    row_iota = jnp.arange(row_count, dtype=jnp.int32)
    taps_rows = taps_table(radius, row_iota[:, None] - row_iota[None, :])
    wide_iota = jnp.arange(3 * col_count, dtype=jnp.int32)
    col_iota = jnp.arange(col_count, dtype=jnp.int32)
    taps_cols = taps_table(radius, wide_iota[:, None] - col_count - col_iota[None, :])
    taps_cols = taps_cols.reshape(lev_dev, 3, col_count, col_count)

    if packed:
        own = spread(level_mix, cell_index, own_keep, radius, col_count, row_count)
    else:
        own = jnp.einsum(
            "kmxy,kyz->kmxz", level_mix, taps_rows, preferred_element_type=jnp.float32
        ).astype(jnp.bfloat16)
    own = jnp.einsum(
        "kmey,kex->kmxy", own, taps_cols[:, 1], preferred_element_type=jnp.float32
    )
    gradient = alpha + own

    sides = jnp.stack([from_left, from_right])
    if packed:
        side_cells = near[0::2]
        sides = jax.vmap(spread, in_axes=(0, 0, 0, None, None, None))(
            sides, side_cells, first_hits(side_cells), radius, col_count, row_count
        )
    else:
        sides = jnp.einsum(
            "tkmxy,kyz->tkmxz", sides, taps_rows, preferred_element_type=jnp.float32
        ).astype(jnp.bfloat16)
    smooth_x = jnp.einsum(
        "tkmey,ktex->kmxy", sides, taps_cols[:, 0::2], preferred_element_type=jnp.float32
    )
    gradient = gradient + smooth_x
    total_cells = float(lev_dev * group_count * col_count * tile_count * row_count)
    gram_local = (
        gram_of(gradient) / total_cells
    )
    gram_total = all_sum(gram_local, (("lev", group_count), ("tile", tile_count)))
    r_factor = jnp.linalg.cholesky(gram_total).T
    return (gradient, r_factor)


def solution(mesh):
    return jax.shard_map(
        shards,
        mesh=mesh,
        in_specs=(
            P("lev", "tile"),
            P("tile", None, None),
            P("tile", None, None),
            P("tile", None, None),
            P("tile", None),
            P("lev", None, "tile", None),
            P(),
            P("lev"),
            P("lev", None, "tile", None),
        ),
        out_specs=(P("lev", None, "tile", None), P()),
        check_vma=False,
    )
```

```python
import jax
import jax.numpy as jnp
from jax import lax
from jax.sharding import PartitionSpec as P

HALO = 16


def taps_table(radius, offsets):
    reach_max = radius.astype(jnp.float32)[:, None, None]
    distance = jnp.abs(offsets).astype(jnp.float32)[None]
    weights = jnp.where(
        distance <= reach_max, (reach_max + 1.0 - distance) / (reach_max + 1.0), 0.0
    )
    return weights.astype(jnp.bfloat16)


def first_hits(cells):
    slots = cells.shape[-1]
    same = cells[..., :, None] == cells[..., None, :]
    later = lax.broadcasted_iota(jnp.int32, (slots, slots), 1) < lax.broadcasted_iota(
        jnp.int32, (slots, slots), 0
    )
    return jnp.logical_not(jnp.any(same & later, axis=-1))


def one_hot(cells, keep, cell_count):
    grid = lax.broadcasted_iota(jnp.int32, cells.shape + (cell_count,), cells.ndim)
    hit = (cells[..., None] == grid) & keep[..., None]
    return hit.astype(jnp.bfloat16)


def all_sum(value, axes):
    if any(size & (size - 1) for _, size in axes):
        return lax.psum(value, tuple(name for name, _ in axes))
    for name, size in axes:
        bit = 1
        while bit < size:
            value = value + lax.ppermute(value, name, [(i, i ^ bit) for i in range(size)])
            bit *= 2
    return value


def spread(mix, cells, keep, radius, col_count, row_count):
    rows = cells % row_count
    cols = cells // row_count
    offsets = rows[:, None] - jnp.arange(row_count, dtype=jnp.int32)[None, :]
    slot_taps = taps_table(radius, offsets) * keep[None, :, None].astype(jnp.bfloat16)
    col_hit = cols[None, :] == jnp.arange(col_count, dtype=jnp.int32)[:, None]
    placed = jnp.where(col_hit[None, None, None], mix[:, :, :, None, :], 0).astype(jnp.bfloat16)
    out = jnp.einsum(
        "gkmxs,ksz->kgmxz", placed, slot_taps, preferred_element_type=jnp.float32
    ).astype(jnp.bfloat16)
    return out.reshape((out.shape[0], -1) + out.shape[3:])


def halo_of(local_mix, tile_count, group_count, step):
    here = lax.axis_index("lev")
    got = []
    for shift in range(group_count):
        chunk = lax.dynamic_index_in_dim(local_mix, (here + shift) % group_count, 0, keepdims=False)
        pairs = [
            (t * group_count + g, (t + step) * group_count + (g + shift) % group_count)
            for t in range(tile_count)
            if 0 <= t + step < tile_count
            for g in range(group_count)
        ]
        got.append(lax.ppermute(chunk, ("tile", "lev"), pairs))
    order = (here - jnp.arange(group_count, dtype=jnp.int32)) % group_count
    return jnp.take(jnp.stack(got), order, axis=0)


def gram_of(panel):
    high = panel.astype(jnp.bfloat16)
    low = (panel - high.astype(jnp.float32)).astype(jnp.bfloat16)
    members = panel.shape[1]
    parts = jnp.concatenate([high, low], axis=1)
    blocks = jnp.einsum("kpxy,kqxy->pq", parts, parts, preferred_element_type=jnp.float32)
    top, bottom = blocks[:members], blocks[members:]
    return (top[:, :members] + top[:, members:]) + (bottom[:, :members] + bottom[:, members:])


def shards(
    obs_adjoint, foot_obs, foot_cell, foot_weight, counts, ensemble, vert_root, radius, alpha
):
    lev_dev, members, col_count, row_count = alpha.shape
    tile_count = lax.axis_size("tile")
    group_count = lax.axis_size("lev")
    capacity = foot_obs.shape[2]
    cell_count = col_count * row_count
    slots = tile_count * capacity
    packed = slots < cell_count
    share = members // group_count
    assert HALO <= col_count

    slot_index = lax.broadcasted_iota(jnp.int32, (tile_count, capacity), 1)
    live_mask = (slot_index < counts[0][:, None]).astype(jnp.float32)
    obs_hit = foot_obs[0][:, :, None] == lax.broadcasted_iota(
        jnp.int32, (1, 1, obs_adjoint.shape[1]), 2
    )
    values = jnp.einsum(
        "lo,dco->ldc", obs_adjoint, obs_hit.astype(jnp.float32),
        precision=lax.Precision.HIGHEST,
    )
    payload = values * (foot_weight[0] * live_mask)[None]
    own_cells = foot_cell[0]
    prev_cells = jnp.concatenate([own_cells[:1], own_cells[:-1]], axis=0)
    next_cells = jnp.concatenate([own_cells[1:], own_cells[-1:]], axis=0)
    cell_rows = jnp.stack([prev_cells, own_cells, next_cells]).astype(jnp.float32)
    outgoing = jnp.concatenate([payload, cell_rows], axis=0)
    arrived = lax.all_to_all(outgoing, "tile", split_axis=1, concat_axis=1, tiled=True)
    near = arrived[lev_dev:].astype(jnp.int32).reshape(3, slots)
    cell_index = near[1]

    if packed:
        same = (cell_index[:, None] == cell_index[None, :]).astype(jnp.float32)
        forcing = jnp.einsum(
            "ls,st->lt", arrived[:lev_dev].reshape(lev_dev, -1), same,
            precision=lax.Precision.HIGHEST,
        )
        own_keep = first_hits(cell_index)

        def own_hits():
            return one_hot(cell_index, own_keep, cell_count).reshape(slots, col_count, row_count)

        picked = jnp.einsum(
            "lgmxy,sxy->glms", ensemble.reshape(lev_dev, group_count, share, col_count, row_count),
            own_hits(), preferred_element_type=jnp.float32,
        )
        member_forcing = (picked * forcing[None, :, None]).astype(jnp.bfloat16)
    else:
        forcing = jnp.zeros((lev_dev, cell_count), jnp.float32)
        forcing = forcing.at[:, cell_index].add(arrived[:lev_dev].reshape(lev_dev, -1))
        forcing = forcing.reshape(lev_dev, col_count, row_count)
        member_forcing = (ensemble * forcing[:, None]).astype(jnp.bfloat16)
        member_forcing = jnp.swapaxes(
            member_forcing.reshape((lev_dev, group_count, share) + member_forcing.shape[2:]), 0, 1
        )

    regrouped = lax.all_to_all(member_forcing, "lev", split_axis=0, concat_axis=0, tiled=True)
    regrouped = regrouped.reshape((group_count * lev_dev,) + regrouped.shape[2:])
    local_mix = jnp.einsum(
        "lk,lm...->km...", vert_root, regrouped, preferred_element_type=jnp.float32
    ).astype(jnp.bfloat16)
    local_mix = local_mix.reshape((group_count, lev_dev) + local_mix.shape[1:])
    level_mix = lax.all_to_all(local_mix, "lev", split_axis=0, concat_axis=0, tiled=True)
    if not packed:
        level_mix = jnp.swapaxes(level_mix, 0, 1).reshape(
            (lev_dev, members) + level_mix.shape[3:]
        )
    ends = tile_count - 1
    if packed:
        from_left = halo_of(local_mix, tile_count, group_count, 1)
        from_right = halo_of(local_mix, tile_count, group_count, -1)
    else:
        from_left = lax.ppermute(level_mix, "tile", [(i, i + 1) for i in range(ends)])
        from_right = lax.ppermute(level_mix, "tile", [(i + 1, i) for i in range(ends)])
    row_iota = jnp.arange(row_count, dtype=jnp.int32)
    taps_rows = taps_table(radius, row_iota[:, None] - row_iota[None, :])
    wide_iota = jnp.arange(3 * col_count, dtype=jnp.int32)
    col_iota = jnp.arange(col_count, dtype=jnp.int32)
    taps_cols = taps_table(radius, wide_iota[:, None] - col_count - col_iota[None, :])
    taps_cols = taps_cols.reshape(lev_dev, 3, col_count, col_count)

    if packed:
        own = spread(level_mix, cell_index, own_keep, radius, col_count, row_count)
    else:
        own = jnp.einsum(
            "kmxy,kyz->kmxz", level_mix, taps_rows, preferred_element_type=jnp.float32
        ).astype(jnp.bfloat16)
    own = jnp.einsum(
        "kmey,kex->kmxy", own, taps_cols[:, 1], preferred_element_type=jnp.float32
    )
    gradient = alpha + own

    sides = jnp.stack([from_left, from_right])
    if packed:
        side_cells = near[0::2]
        sides = jax.vmap(spread, in_axes=(0, 0, 0, None, None, None))(
            sides, side_cells, first_hits(side_cells), radius, col_count, row_count
        )
    else:
        sides = jnp.einsum(
            "tkmxy,kyz->tkmxz", sides, taps_rows, preferred_element_type=jnp.float32
        ).astype(jnp.bfloat16)
    smooth_x = jnp.einsum(
        "tkmey,ktex->kmxy", sides, taps_cols[:, 0::2], preferred_element_type=jnp.float32
    )
    gradient = gradient + smooth_x
    total_cells = float(lev_dev * group_count * col_count * tile_count * row_count)
    gram_local = (
        gram_of(gradient) / total_cells
    )
    gram_total = all_sum(gram_local, (("lev", group_count), ("tile", tile_count)))
    r_factor = jnp.linalg.cholesky(gram_total).T
    return (gradient, r_factor)


def solution(mesh):
    return jax.shard_map(
        shards,
        mesh=mesh,
        in_specs=(
            P("lev", "tile"),
            P("tile", None, None),
            P("tile", None, None),
            P("tile", None, None),
            P("tile", None),
            P("lev", None, "tile", None),
            P(),
            P("lev"),
            P("lev", None, "tile", None),
        ),
        out_specs=(P("lev", None, "tile", None), P()),
        check_vma=False,
    )
```

```python
import jax
import jax.numpy as jnp
from jax import lax
from jax.sharding import PartitionSpec as P

HALO = 16


def taps_table(radius, offsets):
    reach_max = radius.astype(jnp.float32)[:, None, None]
    distance = jnp.abs(offsets).astype(jnp.float32)[None]
    weights = jnp.where(
        distance <= reach_max, (reach_max + 1.0 - distance) / (reach_max + 1.0), 0.0
    )
    return weights.astype(jnp.bfloat16)


def first_hits(cells):
    slots = cells.shape[-1]
    same = cells[..., :, None] == cells[..., None, :]
    later = lax.broadcasted_iota(jnp.int32, (slots, slots), 1) < lax.broadcasted_iota(
        jnp.int32, (slots, slots), 0
    )
    return jnp.logical_not(jnp.any(same & later, axis=-1))


def one_hot(cells, keep, cell_count):
    grid = lax.broadcasted_iota(jnp.int32, cells.shape + (cell_count,), cells.ndim)
    hit = (cells[..., None] == grid) & keep[..., None]
    return hit.astype(jnp.bfloat16)


def all_sum(value, axes):
    if any(size & (size - 1) for _, size in axes):
        return lax.psum(value, tuple(name for name, _ in axes))
    for name, size in axes:
        bit = 1
        while bit < size:
            value = value + lax.ppermute(value, name, [(i, i ^ bit) for i in range(size)])
            bit *= 2
    return value


def spread(mix, cells, keep, radius, col_count, row_count):
    rows = cells % row_count
    cols = cells // row_count
    offsets = rows[:, None] - jnp.arange(row_count, dtype=jnp.int32)[None, :]
    slot_taps = taps_table(radius, offsets) * keep[None, :, None].astype(jnp.bfloat16)
    col_hit = cols[None, :] == jnp.arange(col_count, dtype=jnp.int32)[:, None]
    placed = jnp.where(col_hit[None, None, None], mix[:, :, :, None, :], 0).astype(jnp.bfloat16)
    out = jnp.einsum(
        "gmkxs,ksz->kgmxz", placed, slot_taps, preferred_element_type=jnp.float32
    ).astype(jnp.bfloat16)
    return out.reshape((out.shape[0], -1) + out.shape[3:])


def gram_of(panel):
    high = panel.astype(jnp.bfloat16)
    low = (panel - high.astype(jnp.float32)).astype(jnp.bfloat16)
    members = panel.shape[1]
    parts = jnp.concatenate([high, low], axis=1)
    blocks = jnp.einsum("kpxy,kqxy->pq", parts, parts, preferred_element_type=jnp.float32)
    top, bottom = blocks[:members], blocks[members:]
    return (top[:, :members] + top[:, members:]) + (bottom[:, :members] + bottom[:, members:])


def shards(
    obs_adjoint, foot_obs, foot_cell, foot_weight, counts, ensemble, vert_root, radius, alpha
):
    lev_dev, members, col_count, row_count = alpha.shape
    tile_count = lax.axis_size("tile")
    group_count = lax.axis_size("lev")
    capacity = foot_obs.shape[2]
    cell_count = col_count * row_count
    slots = tile_count * capacity
    packed = slots < cell_count
    share = members // group_count
    assert HALO <= col_count

    slot_index = lax.broadcasted_iota(jnp.int32, (tile_count, capacity), 1)
    live_mask = (slot_index < counts[0][:, None]).astype(jnp.float32)
    obs_hit = foot_obs[0][:, :, None] == lax.broadcasted_iota(
        jnp.int32, (1, 1, obs_adjoint.shape[1]), 2
    )
    values = jnp.einsum(
        "lo,dco->ldc", obs_adjoint, obs_hit.astype(jnp.float32),
        precision=lax.Precision.HIGHEST,
    )
    payload = values * (foot_weight[0] * live_mask)[None]
    own_cells = foot_cell[0]
    prev_cells = jnp.concatenate([own_cells[:1], own_cells[:-1]], axis=0)
    next_cells = jnp.concatenate([own_cells[1:], own_cells[-1:]], axis=0)
    cell_rows = jnp.stack([prev_cells, own_cells, next_cells]).astype(jnp.float32)
    outgoing = jnp.concatenate([payload, cell_rows], axis=0)
    arrived = lax.all_to_all(outgoing, "tile", split_axis=1, concat_axis=1, tiled=True)
    near = arrived[lev_dev:].astype(jnp.int32).reshape(3, slots)
    cell_index = near[1]

    if packed:
        same = (cell_index[:, None] == cell_index[None, :]).astype(jnp.float32)
        forcing = jnp.einsum(
            "ls,st->lt", arrived[:lev_dev].reshape(lev_dev, -1), same,
            precision=lax.Precision.HIGHEST,
        )
        own_keep = first_hits(cell_index)

        def own_hits():
            return one_hot(cell_index, own_keep, cell_count).reshape(slots, col_count, row_count)

        picked = jnp.einsum(
            "lgmxy,sxy->gmls", ensemble.reshape(lev_dev, group_count, share, col_count, row_count),
            own_hits(), preferred_element_type=jnp.float32,
        )
        member_forcing = (picked * forcing[None, None]).astype(jnp.bfloat16)
    else:
        forcing = jnp.zeros((lev_dev, cell_count), jnp.float32)
        forcing = forcing.at[:, cell_index].add(arrived[:lev_dev].reshape(lev_dev, -1))
        forcing = forcing.reshape(lev_dev, col_count, row_count)
        member_forcing = (ensemble * forcing[:, None]).astype(jnp.bfloat16)
        member_forcing = jnp.moveaxis(
            member_forcing.reshape((lev_dev, group_count, share) + member_forcing.shape[2:]), 0, 2
        )

    regrouped = lax.all_to_all(member_forcing, "lev", split_axis=0, concat_axis=0, tiled=True)
    mixing = vert_root.reshape(group_count, lev_dev, group_count, lev_dev)
    local_mix = jnp.einsum(
        "hml...,hlgk->gmk...", regrouped, mixing, preferred_element_type=jnp.float32
    ).astype(jnp.bfloat16)
    level_mix = lax.all_to_all(local_mix, "lev", split_axis=0, concat_axis=0, tiled=True)
    if not packed:
        level_mix = jnp.moveaxis(level_mix, 2, 0).reshape(
            (lev_dev, members) + level_mix.shape[3:]
        )
    ends = tile_count - 1
    from_left = lax.ppermute(level_mix, "tile", [(i, i + 1) for i in range(ends)])
    from_right = lax.ppermute(level_mix, "tile", [(i + 1, i) for i in range(ends)])
    row_iota = jnp.arange(row_count, dtype=jnp.int32)
    taps_rows = taps_table(radius, row_iota[:, None] - row_iota[None, :])
    wide_iota = jnp.arange(3 * col_count, dtype=jnp.int32)
    col_iota = jnp.arange(col_count, dtype=jnp.int32)
    taps_cols = taps_table(radius, wide_iota[:, None] - col_count - col_iota[None, :])
    taps_cols = taps_cols.reshape(lev_dev, 3, col_count, col_count)

    if packed:
        own = spread(level_mix, cell_index, own_keep, radius, col_count, row_count)
    else:
        own = jnp.einsum(
            "kmxy,kyz->kmxz", level_mix, taps_rows, preferred_element_type=jnp.float32
        ).astype(jnp.bfloat16)
    own = jnp.einsum(
        "kmey,kex->kmxy", own, taps_cols[:, 1], preferred_element_type=jnp.float32
    )
    gradient = alpha + own

    sides = jnp.stack([from_left, from_right])
    if packed:
        side_cells = near[0::2]
        sides = jax.vmap(spread, in_axes=(0, 0, 0, None, None, None))(
            sides, side_cells, first_hits(side_cells), radius, col_count, row_count
        )
    else:
        sides = jnp.einsum(
            "tkmxy,kyz->tkmxz", sides, taps_rows, preferred_element_type=jnp.float32
        ).astype(jnp.bfloat16)
    smooth_x = jnp.einsum(
        "tkmey,ktex->kmxy", sides, taps_cols[:, 0::2], preferred_element_type=jnp.float32
    )
    gradient = gradient + smooth_x
    total_cells = float(lev_dev * group_count * col_count * tile_count * row_count)
    gram_local = (
        gram_of(gradient) / total_cells
    )
    gram_total = all_sum(gram_local, (("lev", group_count), ("tile", tile_count)))
    r_factor = jnp.linalg.cholesky(gram_total).T
    return (gradient, r_factor)


def solution(mesh):
    return jax.shard_map(
        shards,
        mesh=mesh,
        in_specs=(
            P("lev", "tile"),
            P("tile", None, None),
            P("tile", None, None),
            P("tile", None, None),
            P("tile", None),
            P("lev", None, "tile", None),
            P(),
            P("lev"),
            P("lev", None, "tile", None),
        ),
        out_specs=(P("lev", None, "tile", None), P()),
        check_vma=False,
    )
```

```python
import jax
import jax.numpy as jnp
from jax import lax
from jax.sharding import PartitionSpec as P

HALO = 16


def taps_table(radius, offsets):
    reach_max = radius.astype(jnp.float32)[:, None, None]
    distance = jnp.abs(offsets).astype(jnp.float32)[None]
    weights = jnp.where(
        distance <= reach_max, (reach_max + 1.0 - distance) / (reach_max + 1.0), 0.0
    )
    return weights.astype(jnp.bfloat16)


def first_hits(cells):
    slots = cells.shape[-1]
    same = cells[..., :, None] == cells[..., None, :]
    later = lax.broadcasted_iota(jnp.int32, (slots, slots), 1) < lax.broadcasted_iota(
        jnp.int32, (slots, slots), 0
    )
    return jnp.logical_not(jnp.any(same & later, axis=-1))


def one_hot(cells, keep, cell_count):
    grid = lax.broadcasted_iota(jnp.int32, cells.shape + (cell_count,), cells.ndim)
    hit = (cells[..., None] == grid) & keep[..., None]
    return hit.astype(jnp.bfloat16)


def all_sum(value, axes):
    if any(size & (size - 1) for _, size in axes):
        return lax.psum(value, tuple(name for name, _ in axes))
    for name, size in axes:
        bit = 1
        while bit < size:
            value = value + lax.ppermute(value, name, [(i, i ^ bit) for i in range(size)])
            bit *= 2
    return value


def spread(mix, cells, keep, radius, col_count, row_count):
    rows = cells % row_count
    cols = cells // row_count
    offsets = rows[:, None] - jnp.arange(row_count, dtype=jnp.int32)[None, :]
    slot_taps = taps_table(radius, offsets) * keep[None, :, None].astype(jnp.bfloat16)
    col_hit = cols[None, :] == jnp.arange(col_count, dtype=jnp.int32)[:, None]
    placed = jnp.where(col_hit[None, None, None], mix[:, :, :, None, :], 0).astype(jnp.bfloat16)
    out = jnp.einsum(
        "gmkxs,ksz->kgmxz", placed, slot_taps, preferred_element_type=jnp.float32
    ).astype(jnp.bfloat16)
    return out.reshape((out.shape[0], -1) + out.shape[3:])


def gram_of(panel):
    high = panel.astype(jnp.bfloat16)
    low = (panel - high.astype(jnp.float32)).astype(jnp.bfloat16)
    members = panel.shape[1]
    parts = jnp.concatenate([high, low], axis=1)
    blocks = jnp.einsum("kpxy,kqxy->pq", parts, parts, preferred_element_type=jnp.float32)
    top, bottom = blocks[:members], blocks[members:]
    return (top[:, :members] + top[:, members:]) + (bottom[:, :members] + bottom[:, members:])


def shards(
    obs_adjoint, foot_obs, foot_cell, foot_weight, counts, ensemble, vert_root, radius, alpha
):
    lev_dev, members, col_count, row_count = alpha.shape
    tile_count = lax.axis_size("tile")
    group_count = lax.axis_size("lev")
    capacity = foot_obs.shape[2]
    cell_count = col_count * row_count
    slots = tile_count * capacity
    packed = slots < cell_count
    share = members // group_count
    assert HALO <= col_count

    slot_index = lax.broadcasted_iota(jnp.int32, (tile_count, capacity), 1)
    live_mask = (slot_index < counts[0][:, None]).astype(jnp.float32)
    obs_hit = foot_obs[0][:, :, None] == lax.broadcasted_iota(
        jnp.int32, (1, 1, obs_adjoint.shape[1]), 2
    )
    values = jnp.einsum(
        "lo,dco->ldc", obs_adjoint, obs_hit.astype(jnp.float32),
        precision=lax.Precision.HIGHEST,
    )
    payload = values * (foot_weight[0] * live_mask)[None]
    own_cells = foot_cell[0]
    prev_cells = jnp.concatenate([own_cells[:1], own_cells[:-1]], axis=0)
    next_cells = jnp.concatenate([own_cells[1:], own_cells[-1:]], axis=0)
    cell_rows = jnp.stack([prev_cells, own_cells, next_cells]).astype(jnp.float32)
    outgoing = jnp.concatenate([payload, cell_rows], axis=0)
    arrived = lax.all_to_all(outgoing, "tile", split_axis=1, concat_axis=1, tiled=True)
    near = arrived[lev_dev:].astype(jnp.int32).reshape(3, slots)
    cell_index = near[1]

    if packed:
        same = (cell_index[:, None] == cell_index[None, :]).astype(jnp.float32)
        forcing = jnp.einsum(
            "ls,st->lt", arrived[:lev_dev].reshape(lev_dev, -1), same,
            precision=lax.Precision.HIGHEST,
        )
        own_keep = first_hits(cell_index)

        def own_hits():
            return one_hot(cell_index, own_keep, cell_count).reshape(slots, col_count, row_count)

        picked = jnp.einsum(
            "lgmxy,sxy->gmls", ensemble.reshape(lev_dev, group_count, share, col_count, row_count),
            own_hits(), preferred_element_type=jnp.float32,
        )
        member_forcing = (picked * forcing[None, None]).astype(jnp.bfloat16)
    else:
        forcing = jnp.zeros((lev_dev, cell_count), jnp.float32)
        forcing = forcing.at[:, cell_index].add(arrived[:lev_dev].reshape(lev_dev, -1))
        forcing = forcing.reshape(lev_dev, col_count, row_count)
        member_forcing = (ensemble * forcing[:, None]).astype(jnp.bfloat16)
        member_forcing = jnp.moveaxis(
            member_forcing.reshape((lev_dev, group_count, share) + member_forcing.shape[2:]), 0, 2
        )

    regrouped = lax.all_to_all(member_forcing, "lev", split_axis=0, concat_axis=0, tiled=True)
    mixing = vert_root.reshape(group_count, lev_dev, group_count, lev_dev)
    local_mix = jnp.einsum(
        "hml...,hlgk->gmk...", regrouped, mixing, preferred_element_type=jnp.float32
    ).astype(jnp.bfloat16)
    level_mix = lax.all_to_all(local_mix, "lev", split_axis=0, concat_axis=0, tiled=True)
    if not packed:
        level_mix = jnp.moveaxis(level_mix, 2, 0).reshape(
            (lev_dev, members) + level_mix.shape[3:]
        )
    ends = tile_count - 1
    from_left = lax.ppermute(level_mix, "tile", [(i, i + 1) for i in range(ends)])
    from_right = lax.ppermute(level_mix, "tile", [(i + 1, i) for i in range(ends)])
    row_iota = jnp.arange(row_count, dtype=jnp.int32)
    taps_rows = taps_table(radius, row_iota[:, None] - row_iota[None, :])
    wide_iota = jnp.arange(3 * col_count, dtype=jnp.int32)
    col_iota = jnp.arange(col_count, dtype=jnp.int32)
    taps_cols = taps_table(radius, wide_iota[:, None] - col_count - col_iota[None, :])
    taps_cols = taps_cols.reshape(lev_dev, 3, col_count, col_count)

    if packed:
        own = spread(level_mix, cell_index, own_keep, radius, col_count, row_count)
    else:
        own = jnp.einsum(
            "kmxy,kyz->kmxz", level_mix, taps_rows, preferred_element_type=jnp.float32
        ).astype(jnp.bfloat16)
    own = jnp.einsum(
        "kmey,kex->kmxy", own, taps_cols[:, 1], preferred_element_type=jnp.float32
    )
    gradient = alpha + own

    if packed:
        left = spread(from_left, near[0], first_hits(near[0]), radius, col_count, row_count)
        right = spread(from_right, near[2], first_hits(near[2]), radius, col_count, row_count)
    else:
        left, right = (
            jnp.einsum(
                "kmxy,kyz->kmxz", side, taps_rows, preferred_element_type=jnp.float32
            ).astype(jnp.bfloat16)
            for side in (from_left, from_right)
        )
    smooth_x = jnp.einsum(
        "kmey,kex->kmxy", left, taps_cols[:, 0], preferred_element_type=jnp.float32
    ) + jnp.einsum(
        "kmey,kex->kmxy", right, taps_cols[:, 2], preferred_element_type=jnp.float32
    )
    gradient = gradient + smooth_x
    total_cells = float(lev_dev * group_count * col_count * tile_count * row_count)
    gram_local = (
        gram_of(gradient) / total_cells
    )
    gram_total = all_sum(gram_local, (("lev", group_count), ("tile", tile_count)))
    r_factor = jnp.linalg.cholesky(gram_total).T
    return (gradient, r_factor)


def solution(mesh):
    return jax.shard_map(
        shards,
        mesh=mesh,
        in_specs=(
            P("lev", "tile"),
            P("tile", None, None),
            P("tile", None, None),
            P("tile", None, None),
            P("tile", None),
            P("lev", None, "tile", None),
            P(),
            P("lev"),
            P("lev", None, "tile", None),
        ),
        out_specs=(P("lev", None, "tile", None), P()),
        check_vma=False,
    )
```

```python
import jax
import jax.numpy as jnp
from jax import lax
from jax.sharding import PartitionSpec as P

HALO = 16


def taps_table(radius, offsets):
    reach_max = radius.astype(jnp.float32)[:, None, None]
    distance = jnp.abs(offsets).astype(jnp.float32)[None]
    weights = jnp.where(
        distance <= reach_max, (reach_max + 1.0 - distance) / (reach_max + 1.0), 0.0
    )
    return weights.astype(jnp.bfloat16)


def first_hits(cells):
    slots = cells.shape[-1]
    same = cells[..., :, None] == cells[..., None, :]
    later = lax.broadcasted_iota(jnp.int32, (slots, slots), 1) < lax.broadcasted_iota(
        jnp.int32, (slots, slots), 0
    )
    return jnp.logical_not(jnp.any(same & later, axis=-1))


def one_hot(cells, keep, cell_count):
    grid = lax.broadcasted_iota(jnp.int32, cells.shape + (cell_count,), cells.ndim)
    hit = (cells[..., None] == grid) & keep[..., None]
    return hit.astype(jnp.bfloat16)


def all_sum(value, axes):
    if any(size & (size - 1) for _, size in axes):
        return lax.psum(value, tuple(name for name, _ in axes))
    for name, size in axes:
        bit = 1
        while bit < size:
            value = value + lax.ppermute(value, name, [(i, i ^ bit) for i in range(size)])
            bit *= 2
    return value


def spread(mix, cells, keep, radius, col_count, row_count):
    rows = cells % row_count
    cols = cells // row_count
    offsets = rows[:, None] - jnp.arange(row_count, dtype=jnp.int32)[None, :]
    slot_taps = taps_table(radius, offsets) * keep[None, :, None].astype(jnp.bfloat16)
    col_hit = cols[None, :] == jnp.arange(col_count, dtype=jnp.int32)[:, None]
    placed = jnp.where(col_hit[None, None, None], mix[:, :, :, None, :], 0).astype(jnp.bfloat16)
    out = jnp.einsum(
        "gmkxs,ksz->kgmxz", placed, slot_taps, preferred_element_type=jnp.float32
    ).astype(jnp.bfloat16)
    return out.reshape((out.shape[0], -1) + out.shape[3:])


def gram_of(panel):
    high = panel.astype(jnp.bfloat16)
    low = (panel - high.astype(jnp.float32)).astype(jnp.bfloat16)
    members = panel.shape[1]
    parts = jnp.concatenate([high, low], axis=1)
    blocks = jnp.einsum("kpxy,kqxy->pq", parts, parts, preferred_element_type=jnp.float32)
    top, bottom = blocks[:members], blocks[members:]
    return (top[:, :members] + top[:, members:]) + (bottom[:, :members] + bottom[:, members:])


def shards(
    obs_adjoint, foot_obs, foot_cell, foot_weight, counts, ensemble, vert_root, radius, alpha
):
    lev_dev, members, col_count, row_count = alpha.shape
    tile_count = lax.axis_size("tile")
    group_count = lax.axis_size("lev")
    capacity = foot_obs.shape[2]
    cell_count = col_count * row_count
    slots = tile_count * capacity
    packed = slots < cell_count
    share = members // group_count
    assert HALO <= col_count

    slot_index = lax.broadcasted_iota(jnp.int32, (tile_count, capacity), 1)
    live_mask = (slot_index < counts[0][:, None]).astype(jnp.float32)
    obs_hit = foot_obs[0][:, :, None] == lax.broadcasted_iota(
        jnp.int32, (1, 1, obs_adjoint.shape[1]), 2
    )
    values = jnp.einsum(
        "lo,dco->ldc", obs_adjoint, obs_hit.astype(jnp.float32),
        precision=lax.Precision.HIGHEST,
    )
    payload = values * (foot_weight[0] * live_mask)[None]
    dest = jnp.arange(tile_count, dtype=jnp.int32)
    beside = jnp.clip(dest[None, :] + jnp.arange(-1, 2, dtype=jnp.int32)[:, None], 0, tile_count - 1)
    near_rows = (beside[:, :, None] == dest[None, None, :]).astype(jnp.float32)
    cell_rows = jnp.einsum(
        "jde,ec->jdc", near_rows, foot_cell[0].astype(jnp.float32),
        precision=lax.Precision.HIGHEST,
    )
    outgoing = jnp.concatenate([payload, cell_rows], axis=0)
    arrived = lax.all_to_all(outgoing, "tile", split_axis=1, concat_axis=1, tiled=True)
    near = arrived[lev_dev:].astype(jnp.int32).reshape(3, slots)
    cell_index = near[1]

    if packed:
        same = (cell_index[:, None] == cell_index[None, :]).astype(jnp.float32)
        forcing = jnp.einsum(
            "ls,st->lt", arrived[:lev_dev].reshape(lev_dev, -1), same,
            precision=lax.Precision.HIGHEST,
        )
        own_keep = first_hits(cell_index)

        def own_hits():
            return one_hot(cell_index, own_keep, cell_count).reshape(slots, col_count, row_count)

        picked = jnp.einsum(
            "lgmxy,sxy->gmls", ensemble.reshape(lev_dev, group_count, share, col_count, row_count),
            own_hits(), preferred_element_type=jnp.float32,
        )
        member_forcing = (picked * forcing[None, None]).astype(jnp.bfloat16)
    else:
        forcing = jnp.zeros((lev_dev, cell_count), jnp.float32)
        forcing = forcing.at[:, cell_index].add(arrived[:lev_dev].reshape(lev_dev, -1))
        forcing = forcing.reshape(lev_dev, col_count, row_count)
        member_forcing = (ensemble * forcing[:, None]).astype(jnp.bfloat16)
        member_forcing = jnp.moveaxis(
            member_forcing.reshape((lev_dev, group_count, share) + member_forcing.shape[2:]), 0, 2
        )

    regrouped = lax.all_to_all(member_forcing, "lev", split_axis=0, concat_axis=0, tiled=True)
    mixing = vert_root.reshape(group_count, lev_dev, group_count, lev_dev)
    local_mix = jnp.einsum(
        "hml...,hlgk->gmk...", regrouped, mixing, preferred_element_type=jnp.float32
    ).astype(jnp.bfloat16)
    level_mix = lax.all_to_all(local_mix, "lev", split_axis=0, concat_axis=0, tiled=True)
    if not packed:
        level_mix = jnp.moveaxis(level_mix, 2, 0).reshape(
            (lev_dev, members) + level_mix.shape[3:]
        )
    ends = tile_count - 1
    from_left = lax.ppermute(level_mix, "tile", [(i, i + 1) for i in range(ends)])
    from_right = lax.ppermute(level_mix, "tile", [(i + 1, i) for i in range(ends)])
    row_iota = jnp.arange(row_count, dtype=jnp.int32)
    taps_rows = taps_table(radius, row_iota[:, None] - row_iota[None, :])
    wide_iota = jnp.arange(3 * col_count, dtype=jnp.int32)
    col_iota = jnp.arange(col_count, dtype=jnp.int32)
    taps_cols = taps_table(radius, wide_iota[:, None] - col_count - col_iota[None, :])
    taps_cols = taps_cols.reshape(lev_dev, 3, col_count, col_count)

    if packed:
        own = spread(level_mix, cell_index, own_keep, radius, col_count, row_count)
    else:
        own = jnp.einsum(
            "kmxy,kyz->kmxz", level_mix, taps_rows, preferred_element_type=jnp.float32
        ).astype(jnp.bfloat16)
    own = jnp.einsum(
        "kmey,kex->kmxy", own, taps_cols[:, 1], preferred_element_type=jnp.float32
    )
    gradient = alpha + own

    if packed:
        left = spread(from_left, near[0], first_hits(near[0]), radius, col_count, row_count)
        right = spread(from_right, near[2], first_hits(near[2]), radius, col_count, row_count)
    else:
        left, right = (
            jnp.einsum(
                "kmxy,kyz->kmxz", side, taps_rows, preferred_element_type=jnp.float32
            ).astype(jnp.bfloat16)
            for side in (from_left, from_right)
        )
    smooth_x = jnp.einsum(
        "kmey,kex->kmxy", left, taps_cols[:, 0], preferred_element_type=jnp.float32
    ) + jnp.einsum(
        "kmey,kex->kmxy", right, taps_cols[:, 2], preferred_element_type=jnp.float32
    )
    gradient = gradient + smooth_x
    total_cells = float(lev_dev * group_count * col_count * tile_count * row_count)
    gram_local = (
        gram_of(gradient) / total_cells
    )
    gram_total = all_sum(gram_local, (("lev", group_count), ("tile", tile_count)))
    r_factor = jnp.linalg.cholesky(gram_total).T
    return (gradient, r_factor)


def solution(mesh):
    return jax.shard_map(
        shards,
        mesh=mesh,
        in_specs=(
            P("lev", "tile"),
            P("tile", None, None),
            P("tile", None, None),
            P("tile", None, None),
            P("tile", None),
            P("lev", None, "tile", None),
            P(),
            P("lev"),
            P("lev", None, "tile", None),
        ),
        out_specs=(P("lev", None, "tile", None), P()),
        check_vma=False,
    )
```

```python
import jax
import jax.numpy as jnp
from jax import lax
from jax.sharding import PartitionSpec as P

HALO = 16


def taps_table(radius, offsets):
    reach_max = radius.astype(jnp.float32)[:, None, None]
    distance = jnp.abs(offsets).astype(jnp.float32)[None]
    weights = jnp.where(
        distance <= reach_max, (reach_max + 1.0 - distance) / (reach_max + 1.0), 0.0
    )
    return weights.astype(jnp.bfloat16)


def first_hits(cells):
    slots = cells.shape[-1]
    same = cells[..., :, None] == cells[..., None, :]
    later = lax.broadcasted_iota(jnp.int32, (slots, slots), 1) < lax.broadcasted_iota(
        jnp.int32, (slots, slots), 0
    )
    return jnp.logical_not(jnp.any(same & later, axis=-1))


def one_hot(cells, keep, cell_count):
    grid = lax.broadcasted_iota(jnp.int32, cells.shape + (cell_count,), cells.ndim)
    hit = (cells[..., None] == grid) & keep[..., None]
    return hit.astype(jnp.bfloat16)


def all_sum(value, axes):
    if any(size & (size - 1) for _, size in axes):
        return lax.psum(value, tuple(name for name, _ in axes))
    for name, size in axes:
        bit = 1
        while bit < size:
            value = value + lax.ppermute(value, name, [(i, i ^ bit) for i in range(size)])
            bit *= 2
    return value


def spread(mix, cells, keep, radius, col_count, row_count):
    rows = cells % row_count
    cols = cells // row_count
    offsets = rows[:, None] - jnp.arange(row_count, dtype=jnp.int32)[None, :]
    slot_taps = taps_table(radius, offsets) * keep[None, :, None].astype(jnp.bfloat16)
    col_hit = cols[None, :] == jnp.arange(col_count, dtype=jnp.int32)[:, None]
    placed = jnp.where(col_hit[None, None, None], mix[:, :, :, None, :], 0).astype(jnp.bfloat16)
    out = jnp.einsum(
        "gmkxs,ksz->kgmxz", placed, slot_taps, preferred_element_type=jnp.float32
    ).astype(jnp.bfloat16)
    return out.reshape((out.shape[0], -1) + out.shape[3:])


def gram_of(panel):
    high = panel.astype(jnp.bfloat16)
    low = (panel - high.astype(jnp.float32)).astype(jnp.bfloat16)
    members = panel.shape[1]
    parts = jnp.concatenate([high, low], axis=1)
    blocks = jnp.einsum("kpxy,kqxy->pq", parts, parts, preferred_element_type=jnp.float32)
    top, bottom = blocks[:members], blocks[members:]
    return (top[:, :members] + top[:, members:]) + (bottom[:, :members] + bottom[:, members:])


def shards(
    obs_adjoint, foot_obs, foot_cell, foot_weight, counts, ensemble, vert_root, radius, alpha
):
    lev_dev, members, col_count, row_count = alpha.shape
    tile_count = lax.axis_size("tile")
    group_count = lax.axis_size("lev")
    capacity = foot_obs.shape[2]
    cell_count = col_count * row_count
    slots = tile_count * capacity
    packed = slots < cell_count
    share = members // group_count
    assert HALO <= col_count

    slot_index = lax.broadcasted_iota(jnp.int32, (tile_count, capacity), 1)
    live_mask = (slot_index < counts[0][:, None]).astype(jnp.float32)
    obs_hit = foot_obs[0][:, :, None] == lax.broadcasted_iota(
        jnp.int32, (1, 1, obs_adjoint.shape[1]), 2
    )
    values = jnp.einsum(
        "lo,dco->ldc", obs_adjoint, obs_hit.astype(jnp.float32),
        precision=lax.Precision.HIGHEST,
    )
    payload = values * (foot_weight[0] * live_mask)[None]
    dest = jnp.arange(tile_count, dtype=jnp.int32)
    beside = jnp.clip(dest[None, :] + jnp.arange(-1, 2, dtype=jnp.int32)[:, None], 0, tile_count - 1)
    near_rows = (beside[:, :, None] == dest[None, None, :]).astype(jnp.float32)
    cell_rows = jnp.einsum(
        "jde,ec->jdc", near_rows, foot_cell[0].astype(jnp.float32),
        precision=lax.Precision.HIGHEST,
    )
    outgoing = jnp.swapaxes(jnp.concatenate([payload, cell_rows], axis=0), 0, 1)
    arrived = lax.all_to_all(outgoing, "tile", split_axis=0, concat_axis=0, tiled=True)
    arrived = jnp.swapaxes(arrived, 0, 1)
    near = arrived[lev_dev:].astype(jnp.int32).reshape(3, slots)
    cell_index = near[1]

    if packed:
        same = (cell_index[:, None] == cell_index[None, :]).astype(jnp.float32)
        forcing = jnp.einsum(
            "ls,st->lt", arrived[:lev_dev].reshape(lev_dev, -1), same,
            precision=lax.Precision.HIGHEST,
        )
        own_keep = first_hits(cell_index)

        def own_hits():
            return one_hot(cell_index, own_keep, cell_count).reshape(slots, col_count, row_count)

        picked = jnp.einsum(
            "lgmxy,sxy->gmls", ensemble.reshape(lev_dev, group_count, share, col_count, row_count),
            own_hits(), preferred_element_type=jnp.float32,
        )
        member_forcing = (picked * forcing[None, None]).astype(jnp.bfloat16)
    else:
        forcing = jnp.zeros((lev_dev, cell_count), jnp.float32)
        forcing = forcing.at[:, cell_index].add(arrived[:lev_dev].reshape(lev_dev, -1))
        forcing = forcing.reshape(lev_dev, col_count, row_count)
        member_forcing = (ensemble * forcing[:, None]).astype(jnp.bfloat16)
        member_forcing = jnp.moveaxis(
            member_forcing.reshape((lev_dev, group_count, share) + member_forcing.shape[2:]), 0, 2
        )

    regrouped = lax.all_to_all(member_forcing, "lev", split_axis=0, concat_axis=0, tiled=True)
    mixing = vert_root.reshape(group_count, lev_dev, group_count, lev_dev)
    local_mix = jnp.einsum(
        "hml...,hlgk->gmk...", regrouped, mixing, preferred_element_type=jnp.float32
    ).astype(jnp.bfloat16)
    level_mix = lax.all_to_all(local_mix, "lev", split_axis=0, concat_axis=0, tiled=True)
    if not packed:
        level_mix = jnp.moveaxis(level_mix, 2, 0).reshape(
            (lev_dev, members) + level_mix.shape[3:]
        )
    ends = tile_count - 1
    from_left = lax.ppermute(level_mix, "tile", [(i, i + 1) for i in range(ends)])
    from_right = lax.ppermute(level_mix, "tile", [(i + 1, i) for i in range(ends)])
    row_iota = jnp.arange(row_count, dtype=jnp.int32)
    taps_rows = taps_table(radius, row_iota[:, None] - row_iota[None, :])
    wide_iota = jnp.arange(3 * col_count, dtype=jnp.int32)
    col_iota = jnp.arange(col_count, dtype=jnp.int32)
    taps_cols = taps_table(radius, wide_iota[:, None] - col_count - col_iota[None, :])
    taps_cols = taps_cols.reshape(lev_dev, 3, col_count, col_count)

    if packed:
        own = spread(level_mix, cell_index, own_keep, radius, col_count, row_count)
    else:
        own = jnp.einsum(
            "kmxy,kyz->kmxz", level_mix, taps_rows, preferred_element_type=jnp.float32
        ).astype(jnp.bfloat16)
    own = jnp.einsum(
        "kmey,kex->kmxy", own, taps_cols[:, 1], preferred_element_type=jnp.float32
    )
    gradient = alpha + own

    if packed:
        left = spread(from_left, near[0], first_hits(near[0]), radius, col_count, row_count)
        right = spread(from_right, near[2], first_hits(near[2]), radius, col_count, row_count)
    else:
        left, right = (
            jnp.einsum(
                "kmxy,kyz->kmxz", side, taps_rows, preferred_element_type=jnp.float32
            ).astype(jnp.bfloat16)
            for side in (from_left, from_right)
        )
    smooth_x = jnp.einsum(
        "kmey,kex->kmxy", left, taps_cols[:, 0], preferred_element_type=jnp.float32
    ) + jnp.einsum(
        "kmey,kex->kmxy", right, taps_cols[:, 2], preferred_element_type=jnp.float32
    )
    gradient = gradient + smooth_x
    total_cells = float(lev_dev * group_count * col_count * tile_count * row_count)
    gram_local = (
        gram_of(gradient) / total_cells
    )
    gram_total = all_sum(gram_local, (("lev", group_count), ("tile", tile_count)))
    r_factor = jnp.linalg.cholesky(gram_total).T
    return (gradient, r_factor)


def solution(mesh):
    return jax.shard_map(
        shards,
        mesh=mesh,
        in_specs=(
            P("lev", "tile"),
            P("tile", None, None),
            P("tile", None, None),
            P("tile", None, None),
            P("tile", None),
            P("lev", None, "tile", None),
            P(),
            P("lev"),
            P("lev", None, "tile", None),
        ),
        out_specs=(P("lev", None, "tile", None), P()),
        check_vma=False,
    )
```

```python
import jax
import jax.numpy as jnp
from jax import lax
from jax.sharding import PartitionSpec as P

HALO = 16


def taps_table(radius, offsets):
    reach_max = radius.astype(jnp.float32)[:, None, None]
    distance = jnp.abs(offsets).astype(jnp.float32)[None]
    weights = jnp.where(
        distance <= reach_max, (reach_max + 1.0 - distance) / (reach_max + 1.0), 0.0
    )
    return weights.astype(jnp.bfloat16)


def first_hits(cells):
    slots = cells.shape[-1]
    same = cells[..., :, None] == cells[..., None, :]
    later = lax.broadcasted_iota(jnp.int32, (slots, slots), 1) < lax.broadcasted_iota(
        jnp.int32, (slots, slots), 0
    )
    return jnp.logical_not(jnp.any(same & later, axis=-1))


def one_hot(cells, keep, cell_count):
    grid = lax.broadcasted_iota(jnp.int32, cells.shape + (cell_count,), cells.ndim)
    hit = (cells[..., None] == grid) & keep[..., None]
    return hit.astype(jnp.bfloat16)


def all_sum(value, axes):
    if any(size & (size - 1) for _, size in axes):
        return lax.psum(value, tuple(name for name, _ in axes))
    for name, size in axes:
        bit = 1
        while bit < size:
            value = value + lax.ppermute(value, name, [(i, i ^ bit) for i in range(size)])
            bit *= 2
    return value


def spread(mix, cells, keep, radius, col_count, row_count):
    rows = cells % row_count
    cols = cells // row_count
    offsets = rows[:, None] - jnp.arange(row_count, dtype=jnp.int32)[None, :]
    slot_taps = taps_table(radius, offsets) * keep[None, :, None].astype(jnp.bfloat16)
    col_hit = cols[None, :] == jnp.arange(col_count, dtype=jnp.int32)[:, None]
    placed = jnp.where(col_hit[None, None, None], mix[:, :, :, None, :], 0).astype(jnp.bfloat16)
    out = jnp.einsum(
        "gmkxs,ksz->kgmxz", placed, slot_taps, preferred_element_type=jnp.float32
    ).astype(jnp.bfloat16)
    return out.reshape((out.shape[0], -1) + out.shape[3:])


def gram_of(panel):
    high = panel.astype(jnp.bfloat16)
    low = (panel - high.astype(jnp.float32)).astype(jnp.bfloat16)
    members = panel.shape[1]
    parts = jnp.concatenate([jnp.swapaxes(high, 0, 1), jnp.swapaxes(low, 0, 1)], axis=0)
    blocks = jnp.einsum("pkxy,qkxy->pq", parts, parts, preferred_element_type=jnp.float32)
    top, bottom = blocks[:members], blocks[members:]
    return (top[:, :members] + top[:, members:]) + (bottom[:, :members] + bottom[:, members:])


def shards(
    obs_adjoint, foot_obs, foot_cell, foot_weight, counts, ensemble, vert_root, radius, alpha
):
    lev_dev, members, col_count, row_count = alpha.shape
    tile_count = lax.axis_size("tile")
    group_count = lax.axis_size("lev")
    capacity = foot_obs.shape[2]
    cell_count = col_count * row_count
    slots = tile_count * capacity
    packed = slots < cell_count
    share = members // group_count
    assert HALO <= col_count

    slot_index = lax.broadcasted_iota(jnp.int32, (tile_count, capacity), 1)
    live_mask = (slot_index < counts[0][:, None]).astype(jnp.float32)
    obs_hit = foot_obs[0][:, :, None] == lax.broadcasted_iota(
        jnp.int32, (1, 1, obs_adjoint.shape[1]), 2
    )
    values = jnp.einsum(
        "lo,dco->ldc", obs_adjoint, obs_hit.astype(jnp.float32),
        precision=lax.Precision.HIGHEST,
    )
    payload = values * (foot_weight[0] * live_mask)[None]
    dest = jnp.arange(tile_count, dtype=jnp.int32)
    beside = jnp.clip(dest[None, :] + jnp.arange(-1, 2, dtype=jnp.int32)[:, None], 0, tile_count - 1)
    near_rows = (beside[:, :, None] == dest[None, None, :]).astype(jnp.float32)
    cell_rows = jnp.einsum(
        "jde,ec->jdc", near_rows, foot_cell[0].astype(jnp.float32),
        precision=lax.Precision.HIGHEST,
    )
    outgoing = jnp.concatenate([payload, cell_rows], axis=0)
    arrived = lax.all_to_all(outgoing, "tile", split_axis=1, concat_axis=1, tiled=True)
    near = arrived[lev_dev:].astype(jnp.int32).reshape(3, slots)
    cell_index = near[1]

    if packed:
        same = (cell_index[:, None] == cell_index[None, :]).astype(jnp.float32)
        forcing = jnp.einsum(
            "ls,st->lt", arrived[:lev_dev].reshape(lev_dev, -1), same,
            precision=lax.Precision.HIGHEST,
        )
        own_keep = first_hits(cell_index)

        def own_hits():
            return one_hot(cell_index, own_keep, cell_count).reshape(slots, col_count, row_count)

        picked = jnp.einsum(
            "lgmxy,sxy->gmls", ensemble.reshape(lev_dev, group_count, share, col_count, row_count),
            own_hits(), preferred_element_type=jnp.float32,
        )
        member_forcing = (picked * forcing[None, None]).astype(jnp.bfloat16)
    else:
        forcing = jnp.zeros((lev_dev, cell_count), jnp.float32)
        forcing = forcing.at[:, cell_index].add(arrived[:lev_dev].reshape(lev_dev, -1))
        forcing = forcing.reshape(lev_dev, col_count, row_count)
        member_forcing = (ensemble * forcing[:, None]).astype(jnp.bfloat16)
        member_forcing = jnp.moveaxis(
            member_forcing.reshape((lev_dev, group_count, share) + member_forcing.shape[2:]), 0, 2
        )

    regrouped = lax.all_to_all(member_forcing, "lev", split_axis=0, concat_axis=0, tiled=True)
    mixing = vert_root.reshape(group_count, lev_dev, group_count, lev_dev)
    local_mix = jnp.einsum(
        "hml...,hlgk->gmk...", regrouped, mixing, preferred_element_type=jnp.float32
    ).astype(jnp.bfloat16)
    level_mix = lax.all_to_all(local_mix, "lev", split_axis=0, concat_axis=0, tiled=True)
    if not packed:
        level_mix = jnp.moveaxis(level_mix, 2, 0).reshape(
            (lev_dev, members) + level_mix.shape[3:]
        )
    ends = tile_count - 1
    from_left = lax.ppermute(level_mix, "tile", [(i, i + 1) for i in range(ends)])
    from_right = lax.ppermute(level_mix, "tile", [(i + 1, i) for i in range(ends)])
    row_iota = jnp.arange(row_count, dtype=jnp.int32)
    taps_rows = taps_table(radius, row_iota[:, None] - row_iota[None, :])
    wide_iota = jnp.arange(3 * col_count, dtype=jnp.int32)
    col_iota = jnp.arange(col_count, dtype=jnp.int32)
    taps_cols = taps_table(radius, wide_iota[:, None] - col_count - col_iota[None, :])
    taps_cols = taps_cols.reshape(lev_dev, 3, col_count, col_count)

    if packed:
        own = spread(level_mix, cell_index, own_keep, radius, col_count, row_count)
    else:
        own = jnp.einsum(
            "kmxy,kyz->kmxz", level_mix, taps_rows, preferred_element_type=jnp.float32
        ).astype(jnp.bfloat16)
    own = jnp.einsum(
        "kmey,kex->kmxy", own, taps_cols[:, 1], preferred_element_type=jnp.float32
    )
    gradient = alpha + own

    if packed:
        left = spread(from_left, near[0], first_hits(near[0]), radius, col_count, row_count)
        right = spread(from_right, near[2], first_hits(near[2]), radius, col_count, row_count)
    else:
        left, right = (
            jnp.einsum(
                "kmxy,kyz->kmxz", side, taps_rows, preferred_element_type=jnp.float32
            ).astype(jnp.bfloat16)
            for side in (from_left, from_right)
        )
    smooth_x = jnp.einsum(
        "kmey,kex->kmxy", left, taps_cols[:, 0], preferred_element_type=jnp.float32
    ) + jnp.einsum(
        "kmey,kex->kmxy", right, taps_cols[:, 2], preferred_element_type=jnp.float32
    )
    gradient = gradient + smooth_x
    total_cells = float(lev_dev * group_count * col_count * tile_count * row_count)
    gram_local = (
        gram_of(gradient) / total_cells
    )
    gram_total = all_sum(gram_local, (("lev", group_count), ("tile", tile_count)))
    r_factor = jnp.linalg.cholesky(gram_total).T
    return (gradient, r_factor)


def solution(mesh):
    return jax.shard_map(
        shards,
        mesh=mesh,
        in_specs=(
            P("lev", "tile"),
            P("tile", None, None),
            P("tile", None, None),
            P("tile", None, None),
            P("tile", None),
            P("lev", None, "tile", None),
            P(),
            P("lev"),
            P("lev", None, "tile", None),
        ),
        out_specs=(P("lev", None, "tile", None), P()),
        check_vma=False,
    )
```
